256 devices in a mesh: dp: 32 (over z, y), expert: 8 (over x, core).
Axes of the slice: x: 4, y: 4, z: 8, core: 2. Of those that a mesh axis runs over, the one named last changes fastest.
Arguments:
- residual: bfloat16 [2048, 4096], P(('dp', 'expert')), may hold values from -8.2 to 8.2
- queries: bfloat16 [2048, 4096], P('dp', 'expert'), may hold values from -24 to 24
- new_keys: bfloat16 [2048, 1024], P('dp', 'expert'), may hold values from -6 to 6
- new_values: bfloat16 [2048, 1024], P('dp', 'expert'), may hold values from -6 to 6
- cache_keys: bfloat16 [64, 1024, 1024], P('dp', None, 'expert'), may hold values from -8 to 8
- cache_values: bfloat16 [64, 1024, 1024], P('dp', None, 'expert'), may hold values from -6 to 6
- out_weight: bfloat16 [4096, 4096], P('expert', 'dp'), may hold values from -1 to 1
- ffn_gain: float32 [4096], replicated, may hold values from 0.1 to 1.9
- router: bfloat16 [4096, 8], replicated, may hold values from -0.0234375 to 0.0234375
- routes: int32 [2048, 2], P(('dp', 'expert')), may hold values from 0 to 7, all different within a row; in each aligned block of 64 rows (0 to 63, 64 to 127, ...) at most 24 rows name the same one
- w_gate: bfloat16 [8, 4096, 14336], P('expert', None, 'dp'), may hold values from -0.09375 to 0.09375
- w_up: bfloat16 [8, 4096, 14336], P('expert', None, 'dp'), may hold values from -0.09375 to 0.09375
- w_down: bfloat16 [8, 14336, 4096], P('expert', 'dp'), may hold values from -0.046875 to 0.046875
- summary_gain: float32 [4096], P('expert'), may hold values from 0.1 to 1.9
- reduce_scale: float32 [32], P('expert'), may hold values from 0.1 to 30
- assign: int32 [64], replicated, may hold values from 0 to 3
Outputs:
- summary: bfloat16 [64, 4096], P('dp', 'expert')
- reduced: bfloat16 [64, 4096], P('dp', 'expert')
The draws below stay inside these ranges and needn't reach their ends.
Inputs may be any that keep to these rules, and one draw needn't show every extreme that they name: `routes`: each token names 2 different experts and every expert is named by some token; among the tokens of one dp index (aligned blocks of 64 rows) no expert is named by more than 24 tokens, and that bound is reached in some block.
All inputs are finite; a program needn't handle non-finite values.
Results may differ from the reference program's by a relative error of at most 0.017.
Values may be sent and summed in bfloat16 or wider, within the bound.
No kernel may reach another device: no remote copies, remote signals or barrier semaphores. Data moves between devices by JAX's collectives and lax.ppermute only.
A program may use at most 128 MiB of HBM per device.

```python
import math
import jax
import jax.numpy as jnp
import numpy as np
from jax import lax

D = 4096
HEADS = 32
KVH = 8
HD = 128
EXPERTS = 8
FF = 14336
TOPK = 2
WIN = 32
CACHE = 1024
SPAN_DEV = 2
REDUCERS = 4
SPANS = 64
TOKENS = 2048
GROUP_CAP = 24
N_DP = 32


def drawn(key):
    key_query, key_cache = jax.random.split(jax.random.fold_in(key, 29), 2)
    query = jnp.clip(jax.random.normal(key_query, (TOKENS, HEADS * HD), jnp.float32), -6.0, 6.0)
    cache = jnp.clip(jax.random.normal(key_cache, (SPANS, CACHE, KVH * HD), jnp.float32), -6.0, 6.0)
    return (query, cache)


def draw_queries(key, part):
    return drawn(key)[0].astype(jnp.bfloat16)


def draw_cache_keys(key, part):
    return drawn(key)[1].astype(jnp.bfloat16)


def draw_residual(key, part):
    key_base, key_cols = jax.random.split(jax.random.fold_in(key, 11), 2)
    ramp = 0.5 + jnp.arange(D, dtype=jnp.float32) / D
    column = ramp * jnp.exp(jax.random.uniform(key_cols, (D,), jnp.float32, math.log(0.6), math.log(1.6)))
    values = 0.5 * jnp.clip(jax.random.normal(key_base, (TOKENS, D), jnp.float32), -6.0, 6.0) * column
    return values.astype(jnp.bfloat16)


def draw_reduce_scale(key, part):
    low_end = math.log(0.1)
    high_end = math.log(0.3)
    return jnp.exp(jax.random.uniform(jax.random.fold_in(key, 43), (HEADS,), jnp.float32, low_end, high_end))


def with_ends(result, rng, least, top_value):
    spot = [jax.random.randint(jax.random.fold_in(rng, axis), (), 0, length) for axis, length in enumerate(result.shape)]
    main_axis = result.shape.index(max(result.shape))
    neighbour = spot[:main_axis] + [(spot[main_axis] + 1) % result.shape[main_axis]] + spot[main_axis + 1:]
    return result.at[tuple(spot)].set(least).at[tuple(neighbour)].set(top_value)


def shard_levels(stream_key, extent, cuts, smallest, largest):
    def one(position, parts):
        steps = jax.random.uniform(jax.random.fold_in(jax.random.fold_in(stream_key, 6), position), (parts,), jnp.float32, smallest / len(cuts), largest / len(cuts))
        return jnp.repeat(jnp.exp(steps), extent[position] // parts).reshape((-1,) + (1,) * (len(extent) - position - 1))

    factor_of = one(*cuts[0])
    for cut in cuts[1:]:
        factor_of = factor_of * one(*cut)
    return factor_of


def deal_out(own_key, own, number, rows, amount, top, reach, slope):
    order = jax.random.permutation(own_key, amount)
    heavy_load, common = load_shares(amount, rows * top, reach, slope, True), load_shares(amount, rows * top, reach, slope, False)
    places = jnp.arange(amount)

    def named(lengths, turn):
        used = int((lengths > 0).sum())
        fixed = max(1, used // 4)
        passed = fixed + (places - fixed + turn * (used - fixed)) % max(1, amount - fixed)
        return jnp.zeros((amount,), jnp.int32).at[order[jnp.where(places < fixed, places, passed)]].set(jnp.asarray(lengths, jnp.int32))

    lengths = jnp.where(number % 4 == 0, named(heavy_load, number // 4), named(common, number - number // 4 - 1))
    mixed = jax.random.permutation(jax.random.fold_in(own, 3), amount)
    giver, receiver = mixed[0:amount // 2 * 2:2], mixed[1:amount // 2 * 2:2]
    room = jnp.minimum(lengths[giver] - 1, reach - lengths[receiver]) // 2
    room = jnp.where((giver == order[0]) | (receiver == order[0]) | (lengths[receiver] == 0), 0, jnp.maximum(room, 0))
    passed = jax.random.randint(jax.random.fold_in(own, 4), (amount // 2,), 0, 1 << 20) % (room + 1)
    lengths = lengths.at[giver].add(-passed).at[receiver].add(passed)
    labels = jnp.searchsorted(jnp.cumsum(lengths), jnp.arange(rows * top), side="right").astype(jnp.int32)
    grid = labels.reshape(top, rows).T
    grid = grid[jax.random.permutation(jax.random.fold_in(own, 1), rows)]
    turn = jax.random.randint(jax.random.fold_in(own, 2), (rows, 1), 0, top)
    return jnp.take_along_axis(grid, (jnp.arange(top)[None, :] + turn) % top, axis=1)


def load_shares(amount, total, most, skew, full):
    portions = [(1 << 20) // math.isqrt(standing ** skew) + 1 for standing in range(1, amount + 1)]
    largest = most if full else min(most, max(-(-total // amount), total * portions[0] // sum(portions)))
    least = 1 if total - largest >= amount - 1 else 0
    given, surplus = [largest] + [least] * (amount - 1), total - largest - least * (amount - 1)
    while surplus > 0:
        candidates = [i for i in range(1, amount) if given[i] < largest] or [i for i in range(1, amount) if given[i] < most]
        whole, remaining = sum([portions[i] for i in candidates]), surplus
        for i in candidates:
            addition = min(most - given[i], max(1, remaining * portions[i] // whole), surplus)
            given[i] = given[i] + addition
            surplus = surplus - addition
    return np.array(given)


def gaussian(key, shape, scale, bound, cuts=(), kind=jnp.bfloat16):
    loudness = shard_levels(key, shape, cuts, -0.22, 0.18) if cuts else 1.0
    result = jax.random.normal(key, shape, jnp.float32) * scale * loudness
    return jnp.minimum(jnp.maximum(result, -bound), bound).astype(kind)


def setup_inputs(seed: int = 0) -> dict:
    seeds = jax.random.split(jax.random.key(seed), 17)
    residual = draw_residual(jax.random.fold_in(seeds[16], 71), 0)
    queries = draw_queries(jax.random.fold_in(seeds[16], 71), 0)
    new_keys = gaussian(seeds[2], (TOKENS, KVH * HD), 1.0, 6.0, ((0, 32), (1, 8)))
    new_values = gaussian(seeds[3], (TOKENS, KVH * HD), 1.0, 6.0, ((0, 32), (1, 8)))
    cache_keys = draw_cache_keys(jax.random.fold_in(seeds[16], 71), 0)
    cache_values = gaussian(seeds[5], (SPANS, CACHE, KVH * HD), 1.0, 6.0, ((0, 32), (2, 8)))
    out_weight = gaussian(seeds[6], (HEADS * HD, D), HEADS ** -0.5, 1.0, ((0, 8), (1, 32)))
    ffn_gain = jnp.clip(1.0 + 0.18 * jax.random.normal(seeds[7], (D,), jnp.float32), 0.1, 1.9)
    router = gaussian(seeds[8], (D, EXPERTS), (16 * D) ** -0.5, 0.0234375)
    routes_keys = jax.random.split(jax.random.fold_in(seeds[9], 1), TOKENS // (SPAN_DEV * WIN))
    routes_turns = jax.random.permutation(jax.random.fold_in(seeds[9], 3), TOKENS // (SPAN_DEV * WIN))
    routes = jax.vmap(lambda own, number: deal_out(jax.random.fold_in(seeds[9], 2), own, number, SPAN_DEV * WIN, EXPERTS, TOPK, GROUP_CAP, 2))(routes_keys, routes_turns).reshape((TOKENS, TOPK))
    w_gate = gaussian(seeds[10], (EXPERTS, D, FF), D ** -0.5, 0.09375, ((0, 8), (2, 32)))
    w_up = gaussian(seeds[11], (EXPERTS, D, FF), D ** -0.5, 0.09375, ((0, 8), (2, 32)))
    w_down = gaussian(seeds[12], (EXPERTS, FF, D), FF ** -0.5, 0.046875, ((0, 8), (1, 32)))
    summary_gain = jnp.clip(1.0 + 0.18 * jax.random.normal(seeds[13], (D,), jnp.float32), 0.1, 1.9)
    reduce_scale = draw_reduce_scale(jax.random.fold_in(seeds[16], 71), 0)
    assign = with_ends(jax.random.randint(seeds[15], (SPANS,), 0, REDUCERS), jax.random.fold_in(seeds[15], 1), 0, REDUCERS - 1).astype(jnp.int32)
    return {"residual": residual, "queries": queries, "new_keys": new_keys, "new_values": new_values, "cache_keys": cache_keys, "cache_values": cache_values, "out_weight": out_weight, "ffn_gain": ffn_gain, "router": router, "routes": routes, "w_gate": w_gate, "w_up": w_up, "w_down": w_down, "summary_gain": summary_gain, "reduce_scale": reduce_scale, "assign": assign}


EPSILON = 1e-05

def attend(queries, new_keys, new_values, cache_keys, cache_values):
    span_count, cache_len, kv_width = cache_keys.shape
    kv_local = kv_width // HD
    group = HEADS // KVH
    window = queries.shape[0] // span_count
    query_view = queries.reshape(span_count, window, kv_local, group, HD).astype(jnp.float32)
    fresh_keys = new_keys.reshape(span_count, window, kv_local, HD).astype(jnp.float32)
    fresh_values = new_values.reshape(span_count, window, kv_local, HD).astype(jnp.float32)
    stored_keys = cache_keys.reshape(span_count, cache_len, kv_local, HD).astype(jnp.float32)
    stored_values = cache_values.reshape(span_count, cache_len, kv_local, HD).astype(jnp.float32)
    factor = 1.0 / math.sqrt(HD)
    past_scores = jnp.einsum('ctkgd,cpkd->ckgtp', query_view, stored_keys) * factor
    fresh_scores = jnp.einsum('ctkgd,cskd->ckgts', query_view, fresh_keys) * factor
    causal = jnp.arange(window)[:, None] >= jnp.arange(window)[None, :]
    fresh_scores = jnp.where(causal, fresh_scores, -jnp.inf)
    highest = jnp.maximum(lax.optimization_barrier(jnp.max(past_scores, axis=-1)), lax.optimization_barrier(jnp.max(fresh_scores, axis=-1)))[..., None]
    past_exp = jnp.exp(past_scores - highest)
    fresh_exp = jnp.exp(fresh_scores - highest)
    totals = lax.optimization_barrier(jnp.sum(past_exp, axis=-1, keepdims=True)) + lax.optimization_barrier(jnp.sum(fresh_exp, axis=-1, keepdims=True))
    past_weights = (past_exp / totals).astype(jnp.bfloat16).astype(jnp.float32)
    fresh_weights = (fresh_exp / totals).astype(jnp.bfloat16).astype(jnp.float32)
    context = jnp.einsum('ckgtp,cpkd->ctkgd', past_weights, stored_values)
    context = context + jnp.einsum('ckgts,cskd->ctkgd', fresh_weights, fresh_values)
    return context.astype(jnp.bfloat16).reshape(span_count * window, kv_local * group * HD)

def reference(residual, queries, new_keys, new_values, cache_keys, cache_values, out_weight, ffn_gain, router, routes, w_gate, w_up, w_down, summary_gain, reduce_scale, assign):
    per_span = (queries.reshape(SPANS, WIN, HEADS * HD), new_keys.reshape(SPANS, WIN, KVH * HD), new_values.reshape(SPANS, WIN, KVH * HD), cache_keys, cache_values)

    def one_span(items):
        return attend(items[0], items[1], items[2], items[3][None], items[4][None])
    attended = lax.map(one_span, per_span).reshape(TOKENS, HEADS * HD)
    mixed = residual.astype(jnp.float32) + jnp.dot(attended, out_weight, preferred_element_type=jnp.float32)
    normed = (mixed * lax.rsqrt(lax.optimization_barrier(jnp.mean(mixed * mixed, axis=-1, keepdims=True)) + EPSILON) * ffn_gain).astype(jnp.bfloat16)
    logits = jnp.dot(normed, router, preferred_element_type=jnp.float32)
    expert_ids = jnp.arange(EXPERTS, dtype=jnp.int32)
    first = routes[:, 0:1] == expert_ids[None, :]
    second = routes[:, 1:2] == expert_ids[None, :]
    first_logit = lax.optimization_barrier(jnp.sum(jnp.where(first, logits, 0.0), axis=-1))
    second_logit = lax.optimization_barrier(jnp.sum(jnp.where(second, logits, 0.0), axis=-1))
    gates = jnp.stack([jax.nn.sigmoid(first_logit - second_logit), jax.nn.sigmoid(second_logit - first_logit)], axis=1)
    slot_total = N_DP * GROUP_CAP

    def expert_pass(running, expert):
        chosen = routes == expert
        gate_here = lax.optimization_barrier(jnp.sum(jnp.where(chosen, gates, 0.0), axis=1))
        member = jnp.any(chosen, axis=1)
        place = jnp.cumsum(member.astype(jnp.int32)) - 1
        target = jnp.where(member, place, slot_total).astype(jnp.int32)
        index = jnp.zeros((slot_total,), jnp.int32).at[target].set(jnp.arange(TOKENS, dtype=jnp.int32), mode='drop')
        filled = jnp.arange(slot_total, dtype=jnp.int32) < jnp.sum(member.astype(jnp.int32))
        rows = normed[index]
        gate_matrix = lax.dynamic_index_in_dim(w_gate, expert, 0, keepdims=False)
        up_matrix = lax.dynamic_index_in_dim(w_up, expert, 0, keepdims=False)
        down_matrix = lax.dynamic_index_in_dim(w_down, expert, 0, keepdims=False)
        gate_proj = jnp.dot(rows, gate_matrix, preferred_element_type=jnp.float32)
        up_proj = jnp.dot(rows, up_matrix, preferred_element_type=jnp.float32)
        hidden = (jax.nn.silu(gate_proj) * up_proj).astype(jnp.bfloat16)
        outputs = jnp.dot(hidden, down_matrix, preferred_element_type=jnp.float32)
        weight = jnp.where(filled, gate_here[index], 0.0)
        return (running.at[index].add(weight[:, None] * outputs), None)
    moe, unused = lax.scan(expert_pass, jnp.zeros((TOKENS, D), jnp.float32), expert_ids)
    token_out = mixed + moe
    pooled = lax.optimization_barrier(jnp.sum(token_out.reshape(SPANS, WIN, D), axis=1))
    summary = (pooled * lax.rsqrt(lax.optimization_barrier(jnp.mean(pooled * pooled, axis=-1, keepdims=True)) + EPSILON) * summary_gain).astype(jnp.bfloat16)
    heads = summary.reshape(SPANS, HEADS, HD).astype(jnp.float32)
    factor = reduce_scale / math.sqrt(HD)
    scores = jnp.einsum('chd,khd->hck', heads, heads) * factor[:, None, None]
    same = assign[:, None] == assign[None, :]
    scores = jnp.where(same[None], scores, -jnp.inf)
    highest = lax.optimization_barrier(jnp.max(scores, axis=-1, keepdims=True))
    expo = jnp.exp(scores - highest)
    weights = (expo / lax.optimization_barrier(jnp.sum(expo, axis=-1, keepdims=True))).astype(jnp.bfloat16).astype(jnp.float32)
    reduced = jnp.einsum('hck,khd->chd', weights, heads).reshape(SPANS, D).astype(jnp.bfloat16)
    return (summary, reduced)
```

```python
import math

import jax
import jax.numpy as jnp
from jax import lax
from jax.sharding import PartitionSpec as P

HEADS = 32
KVH = 8
HD = 128
EXPERTS = 8
WIN = 32
GROUP_CAP = 24


EPSILON = 1e-05


def attend(queries, new_keys, new_values, cache_keys, cache_values):
    span_count, cache_len, kv_width = cache_keys.shape
    kv_local = kv_width // HD
    group = HEADS // KVH
    window = queries.shape[0] // span_count
    query_view = queries.reshape(span_count, window, kv_local, group, HD)
    fresh_keys = new_keys.reshape(span_count, window, kv_local, HD)
    fresh_values = new_values.reshape(span_count, window, kv_local, HD)
    stored_keys = cache_keys.reshape(span_count, cache_len, kv_local, HD)
    stored_values = cache_values.reshape(span_count, cache_len, kv_local, HD)
    factor = 1.0 / math.sqrt(HD)
    past_scores = (
        jnp.einsum("ctkgd,cpkd->ckgtp", query_view, stored_keys, preferred_element_type=jnp.float32)
        * factor
    )
    fresh_scores = (
        jnp.einsum("ctkgd,cskd->ckgts", query_view, fresh_keys, preferred_element_type=jnp.float32)
        * factor
    )
    causal = jnp.arange(window)[:, None] >= jnp.arange(window)[None, :]
    fresh_scores = jnp.where(causal, fresh_scores, -jnp.inf)
    highest = jnp.maximum(jnp.max(past_scores, axis=-1), jnp.max(fresh_scores, axis=-1))[..., None]
    past_exp = jnp.exp(past_scores - highest)
    fresh_exp = jnp.exp(fresh_scores - highest)
    totals = jnp.sum(past_exp, axis=-1, keepdims=True) + jnp.sum(fresh_exp, axis=-1, keepdims=True)
    past_weights = (past_exp / totals).astype(jnp.bfloat16)
    fresh_weights = (fresh_exp / totals).astype(jnp.bfloat16)
    context = jnp.einsum(
        "ckgtp,cpkd->ctkgd", past_weights, stored_values, preferred_element_type=jnp.float32
    )
    context = context + jnp.einsum(
        "ckgts,cskd->ctkgd", fresh_weights, fresh_values, preferred_element_type=jnp.float32
    )
    return context.astype(jnp.bfloat16).reshape(span_count * window, kv_local * group * HD)


def shards(
    residual,
    queries,
    new_keys,
    new_values,
    cache_keys,
    cache_values,
    out_weight,
    ffn_gain,
    router,
    routes,
    w_gate,
    w_up,
    w_down,
    summary_gain,
    reduce_scale,
    assign,
):
    expert_count = lax.axis_size("expert")
    dp_index = lax.axis_index("dp")
    column = lax.axis_index("expert")
    span_local = cache_keys.shape[0]
    tok_local = residual.shape[0]
    width = residual.shape[1]
    slice_width = width // expert_count
    highest_precision = lax.Precision.HIGHEST
    attended = attend(queries, new_keys, new_values, cache_keys, cache_values)
    head_terms = jnp.dot(
        attended,
        lax.all_gather(out_weight, "dp", axis=1, tiled=True),
        preferred_element_type=jnp.float32,
    )
    mixed = residual.astype(jnp.float32) + lax.psum_scatter(
        head_terms, "expert", scatter_dimension=0, tiled=True
    )
    normed = (
        mixed * lax.rsqrt(jnp.mean(mixed * mixed, axis=-1, keepdims=True) + EPSILON) * ffn_gain
    ).astype(jnp.bfloat16)
    expert_ids = jnp.arange(EXPERTS, dtype=jnp.int32)
    first = routes[:, 0:1] == expert_ids[None, :]
    second = routes[:, 1:2] == expert_ids[None, :]
    partner = jnp.where(first, routes[:, 1:2], jnp.where(second, routes[:, 0:1], -1))
    outgoing = jnp.where((partner >= 0).T[:, :, None], normed[None, :, :], 0)
    arrived_rows, arrived_partner = (
        lax.all_to_all(outgoing, "expert", split_axis=0, concat_axis=1, tiled=True),
        lax.all_to_all(partner.T, "expert", split_axis=0, concat_axis=1, tiled=True),
    )
    present = (arrived_partner >= 0).astype(jnp.int32)
    position = jnp.cumsum(present, axis=1) - 1
    picker = (present[:, None, :] > 0) & (
        position[:, None, :] == jnp.arange(GROUP_CAP)[None, :, None]
    )
    compact = jnp.einsum(
        "eks,esd->ked",
        picker.astype(jnp.bfloat16),
        arrived_rows,
        preferred_element_type=jnp.float32,
    ).astype(jnp.bfloat16)
    arrived_count = arrived_partner.shape[1]
    pick = picker[0]
    slot_present = jnp.any(pick, axis=1)
    slot_partner = jnp.sum(jnp.where(pick, arrived_partner[0][None, :], 0), axis=1)
    local_span = jnp.arange(arrived_count) // WIN
    slot_span = jnp.sum(jnp.where(pick, local_span[None, :], 0), axis=1)
    slot_logits = jnp.dot(compact[:, 0, :], router, preferred_element_type=jnp.float32)
    own_logit = jnp.sum(jnp.where(expert_ids[None, :] == column, slot_logits, 0.0), axis=-1)
    partner_logit = jnp.sum(
        jnp.where(expert_ids[None, :] == slot_partner[:, None], slot_logits, 0.0), axis=-1
    )
    slot_gate = jnp.where(slot_present, jax.nn.sigmoid(own_logit - partner_logit), 0.0)
    pool_weight = jnp.where(
        slot_span[:, None] == jnp.arange(span_local)[None, :], slot_gate[:, None], 0.0
    )
    gathered = lax.all_gather(compact, "dp", axis=0, tiled=True)
    gathered_weight = lax.all_gather(pool_weight, "dp", axis=0, tiled=True)
    n_dp = gathered.shape[0] // GROUP_CAP
    gate_proj = jnp.einsum("ned,edf->nf", gathered, w_gate, preferred_element_type=jnp.float32)
    up_proj = jnp.einsum("ned,edf->nf", gathered, w_up, preferred_element_type=jnp.float32)
    hidden = (jax.nn.silu(gate_proj) * up_proj).astype(jnp.bfloat16)
    span_hidden = jnp.einsum(
        "iks,ikf->isf",
        gathered_weight.reshape(n_dp, GROUP_CAP, span_local),
        hidden.reshape(n_dp, GROUP_CAP, -1).astype(jnp.float32),
        precision=highest_precision,
    ).reshape(n_dp * span_local, -1)
    pooled_part = jnp.dot(
        span_hidden, w_down[0].astype(jnp.float32), precision=highest_precision
    )
    own_span = dp_index * span_local + (column * tok_local) // WIN
    span_count = n_dp * span_local
    mixed_sum = jnp.sum(mixed, axis=0)
    pooled_part = pooled_part + jnp.where(
        (jnp.arange(span_count) == own_span)[:, None], mixed_sum[None, :], 0.0
    )
    pooled_cols = lax.psum_scatter(pooled_part, "expert", scatter_dimension=1, tiled=True)
    pooled_cols = lax.psum(pooled_cols, "dp")
    squares = lax.psum(jnp.sum(pooled_cols * pooled_cols, axis=-1), "expert")
    everyone = (
        pooled_cols * lax.rsqrt(squares / width + EPSILON)[:, None] * summary_gain
    ).astype(jnp.bfloat16)
    summary = lax.dynamic_slice_in_dim(everyone, dp_index * span_local, span_local)
    heads_local = slice_width // HD
    mine = summary.reshape(span_local, heads_local, HD)
    others = everyone.reshape(everyone.shape[0], heads_local, HD)
    factor = reduce_scale / math.sqrt(HD)
    scores = (
        jnp.einsum("chd,khd->hck", mine, others, preferred_element_type=jnp.float32)
        * factor[:, None, None]
    )
    own_assign = lax.dynamic_slice_in_dim(assign, dp_index * span_local, span_local)
    same = own_assign[:, None] == assign[None, :]
    scores = jnp.where(same[None], scores, -jnp.inf)
    highest = jnp.max(scores, axis=-1, keepdims=True)
    expo = jnp.exp(scores - highest)
    weights = (expo / jnp.sum(expo, axis=-1, keepdims=True)).astype(jnp.bfloat16)
    reduced = jnp.einsum("hck,khd->chd", weights, others, preferred_element_type=jnp.float32)
    reduced = reduced.reshape(span_local, slice_width).astype(jnp.bfloat16)
    return (summary, reduced)


def solution(mesh):
    return jax.shard_map(
        shards,
        mesh=mesh,
        in_specs=(
            P(("dp", "expert"), None),
            P("dp", "expert"),
            P("dp", "expert"),
            P("dp", "expert"),
            P("dp", None, "expert"),
            P("dp", None, "expert"),
            P("expert", "dp"),
            P(),
            P(),
            P(("dp", "expert"), None),
            P("expert", None, "dp"),
            P("expert", None, "dp"),
            P("expert", "dp", None),
            P("expert"),
            P("expert"),
            P(),
        ),
        out_specs=(P("dp", "expert"), P("dp", "expert")),
        check_vma=False,
    )
```

```python
import math

import jax
import jax.numpy as jnp
from jax import lax
from jax.sharding import PartitionSpec as P

HEADS = 32
KVH = 8
HD = 128
EXPERTS = 8
WIN = 32
GROUP_CAP = 24


EPSILON = 1e-05


def attend(queries, new_keys, new_values, cache_keys, cache_values):
    span_count, cache_len, kv_width = cache_keys.shape
    kv_local = kv_width // HD
    group = HEADS // KVH
    window = queries.shape[0] // span_count
    query_view = queries.reshape(span_count, window, kv_local, group, HD)
    fresh_keys = new_keys.reshape(span_count, window, kv_local, HD)
    fresh_values = new_values.reshape(span_count, window, kv_local, HD)
    stored_keys = cache_keys.reshape(span_count, cache_len, kv_local, HD)
    stored_values = cache_values.reshape(span_count, cache_len, kv_local, HD)
    factor = 1.0 / math.sqrt(HD)
    past_scores = (
        jnp.einsum("ctkgd,cpkd->ckgtp", query_view, stored_keys, preferred_element_type=jnp.float32)
        * factor
    )
    fresh_scores = (
        jnp.einsum("ctkgd,cskd->ckgts", query_view, fresh_keys, preferred_element_type=jnp.float32)
        * factor
    )
    causal = jnp.arange(window)[:, None] >= jnp.arange(window)[None, :]
    fresh_scores = jnp.where(causal, fresh_scores, -jnp.inf)
    highest = jnp.maximum(jnp.max(past_scores, axis=-1), jnp.max(fresh_scores, axis=-1))[..., None]
    past_exp = jnp.exp(past_scores - highest)
    fresh_exp = jnp.exp(fresh_scores - highest)
    totals = jnp.sum(past_exp, axis=-1, keepdims=True) + jnp.sum(fresh_exp, axis=-1, keepdims=True)
    past_weights = (past_exp / totals).astype(jnp.bfloat16)
    fresh_weights = (fresh_exp / totals).astype(jnp.bfloat16)
    context = jnp.einsum(
        "ckgtp,cpkd->ctkgd", past_weights, stored_values, preferred_element_type=jnp.float32
    )
    context = context + jnp.einsum(
        "ckgts,cskd->ctkgd", fresh_weights, fresh_values, preferred_element_type=jnp.float32
    )
    return context.astype(jnp.bfloat16).reshape(span_count * window, kv_local * group * HD)


def doubling_sum(x, axis, count):
    step = 1
    while step < count:
        x = x + lax.ppermute(x, axis, [(a, a ^ step) for a in range(count)])
        step *= 2
    return x


def shards(
    residual,
    queries,
    new_keys,
    new_values,
    cache_keys,
    cache_values,
    out_weight,
    ffn_gain,
    router,
    routes,
    w_gate,
    w_up,
    w_down,
    summary_gain,
    reduce_scale,
    assign,
):
    expert_count = lax.axis_size("expert")
    dp_index = lax.axis_index("dp")
    column = lax.axis_index("expert")
    span_local = cache_keys.shape[0]
    tok_local = residual.shape[0]
    width = residual.shape[1]
    slice_width = width // expert_count
    highest_precision = lax.Precision.HIGHEST
    attended = attend(queries, new_keys, new_values, cache_keys, cache_values)
    head_terms = jnp.dot(
        attended,
        lax.all_gather(out_weight, "dp", axis=1, tiled=True),
        preferred_element_type=jnp.float32,
    )
    mixed = residual.astype(jnp.float32) + lax.psum_scatter(
        head_terms, "expert", scatter_dimension=0, tiled=True
    )
    normed = (
        mixed * lax.rsqrt(jnp.mean(mixed * mixed, axis=-1, keepdims=True) + EPSILON) * ffn_gain
    ).astype(jnp.bfloat16)
    expert_ids = jnp.arange(EXPERTS, dtype=jnp.int32)
    first = routes[:, 0:1] == expert_ids[None, :]
    second = routes[:, 1:2] == expert_ids[None, :]
    partner = jnp.where(first, routes[:, 1:2], jnp.where(second, routes[:, 0:1], -1))
    outgoing = jnp.where((partner >= 0).T[:, :, None], normed[None, :, :], 0)
    arrived_rows, arrived_partner = (
        lax.all_to_all(outgoing, "expert", split_axis=0, concat_axis=1, tiled=True),
        lax.all_to_all(partner.T, "expert", split_axis=0, concat_axis=1, tiled=True),
    )
    present = (arrived_partner >= 0).astype(jnp.int32)
    position = jnp.cumsum(present, axis=1) - 1
    picker = (present[:, None, :] > 0) & (
        position[:, None, :] == jnp.arange(GROUP_CAP)[None, :, None]
    )
    compact = jnp.einsum(
        "eks,esd->ked",
        picker.astype(jnp.bfloat16),
        arrived_rows,
        preferred_element_type=jnp.float32,
    ).astype(jnp.bfloat16)
    arrived_count = arrived_partner.shape[1]
    pick = picker[0]
    slot_present = jnp.any(pick, axis=1)
    slot_partner = jnp.sum(jnp.where(pick, arrived_partner[0][None, :], 0), axis=1)
    local_span = jnp.arange(arrived_count) // WIN
    slot_span = jnp.sum(jnp.where(pick, local_span[None, :], 0), axis=1)
    slot_logits = jnp.dot(compact[:, 0, :], router, preferred_element_type=jnp.float32)
    own_logit = jnp.sum(jnp.where(expert_ids[None, :] == column, slot_logits, 0.0), axis=-1)
    partner_logit = jnp.sum(
        jnp.where(expert_ids[None, :] == slot_partner[:, None], slot_logits, 0.0), axis=-1
    )
    slot_gate = jnp.where(slot_present, jax.nn.sigmoid(own_logit - partner_logit), 0.0)
    pool_weight = jnp.where(
        slot_span[:, None] == jnp.arange(span_local)[None, :], slot_gate[:, None], 0.0
    )
    gathered = lax.all_gather(compact, "dp", axis=0, tiled=True)
    gathered_weight = lax.all_gather(pool_weight, "dp", axis=0, tiled=True)
    n_dp = gathered.shape[0] // GROUP_CAP
    gate_proj = jnp.einsum("ned,edf->nf", gathered, w_gate, preferred_element_type=jnp.float32)
    up_proj = jnp.einsum("ned,edf->nf", gathered, w_up, preferred_element_type=jnp.float32)
    hidden = (jax.nn.silu(gate_proj) * up_proj).astype(jnp.bfloat16)
    span_hidden = jnp.einsum(
        "iks,ikf->isf",
        gathered_weight.reshape(n_dp, GROUP_CAP, span_local),
        hidden.reshape(n_dp, GROUP_CAP, -1).astype(jnp.float32),
        precision=highest_precision,
    ).reshape(n_dp * span_local, -1)
    pooled_part = jnp.dot(
        span_hidden, w_down[0].astype(jnp.float32), precision=highest_precision
    )
    own_span = dp_index * span_local + (column * tok_local) // WIN
    span_count = n_dp * span_local
    mixed_sum = jnp.sum(mixed, axis=0)
    pooled_part = pooled_part + jnp.where(
        (jnp.arange(span_count) == own_span)[:, None], mixed_sum[None, :], 0.0
    )
    pooled_cols = lax.psum_scatter(pooled_part, "expert", scatter_dimension=1, tiled=True)
    pooled_cols = doubling_sum(pooled_cols, "dp", n_dp)
    squares = doubling_sum(jnp.sum(pooled_cols * pooled_cols, axis=-1), "expert", expert_count)
    everyone = (
        pooled_cols * lax.rsqrt(squares / width + EPSILON)[:, None] * summary_gain
    ).astype(jnp.bfloat16)
    summary = lax.dynamic_slice_in_dim(everyone, dp_index * span_local, span_local)
    heads_local = slice_width // HD
    mine = summary.reshape(span_local, heads_local, HD)
    others = everyone.reshape(everyone.shape[0], heads_local, HD)
    factor = reduce_scale / math.sqrt(HD)
    scores = (
        jnp.einsum("chd,khd->hck", mine, others, preferred_element_type=jnp.float32)
        * factor[:, None, None]
    )
    own_assign = lax.dynamic_slice_in_dim(assign, dp_index * span_local, span_local)
    same = own_assign[:, None] == assign[None, :]
    scores = jnp.where(same[None], scores, -jnp.inf)
    highest = jnp.max(scores, axis=-1, keepdims=True)
    expo = jnp.exp(scores - highest)
    weights = (expo / jnp.sum(expo, axis=-1, keepdims=True)).astype(jnp.bfloat16)
    reduced = jnp.einsum("hck,khd->chd", weights, others, preferred_element_type=jnp.float32)
    reduced = reduced.reshape(span_local, slice_width).astype(jnp.bfloat16)
    return (summary, reduced)


def solution(mesh):
    return jax.shard_map(
        shards,
        mesh=mesh,
        in_specs=(
            P(("dp", "expert"), None),
            P("dp", "expert"),
            P("dp", "expert"),
            P("dp", "expert"),
            P("dp", None, "expert"),
            P("dp", None, "expert"),
            P("expert", "dp"),
            P(),
            P(),
            P(("dp", "expert"), None),
            P("expert", None, "dp"),
            P("expert", None, "dp"),
            P("expert", "dp", None),
            P("expert"),
            P("expert"),
            P(),
        ),
        out_specs=(P("dp", "expert"), P("dp", "expert")),
        check_vma=False,
    )
```

```python
import math

import jax
import jax.numpy as jnp
from jax import lax
from jax.sharding import PartitionSpec as P

HEADS = 32
KVH = 8
HD = 128
EXPERTS = 8
WIN = 32
GROUP_CAP = 24


EPSILON = 1e-05


def attend(queries, new_keys, new_values, cache_keys, cache_values):
    span_count, cache_len, kv_width = cache_keys.shape
    kv_local = kv_width // HD
    group = HEADS // KVH
    window = queries.shape[0] // span_count
    query_view = queries.reshape(span_count, window, kv_local, group, HD)
    fresh_keys = new_keys.reshape(span_count, window, kv_local, HD)
    fresh_values = new_values.reshape(span_count, window, kv_local, HD)
    stored_keys = cache_keys.reshape(span_count, cache_len, kv_local, HD)
    stored_values = cache_values.reshape(span_count, cache_len, kv_local, HD)
    factor = 1.0 / math.sqrt(HD)
    past_scores = (
        jnp.einsum("ctkgd,cpkd->ckgtp", query_view, stored_keys, preferred_element_type=jnp.float32)
        * factor
    )
    fresh_scores = (
        jnp.einsum("ctkgd,cskd->ckgts", query_view, fresh_keys, preferred_element_type=jnp.float32)
        * factor
    )
    causal = jnp.arange(window)[:, None] >= jnp.arange(window)[None, :]
    fresh_scores = jnp.where(causal, fresh_scores, -jnp.inf)
    highest = jnp.maximum(jnp.max(past_scores, axis=-1), jnp.max(fresh_scores, axis=-1))[..., None]
    past_exp = jnp.exp(past_scores - highest)
    fresh_exp = jnp.exp(fresh_scores - highest)
    totals = jnp.sum(past_exp, axis=-1, keepdims=True) + jnp.sum(fresh_exp, axis=-1, keepdims=True)
    past_weights = (past_exp / totals).astype(jnp.bfloat16)
    fresh_weights = (fresh_exp / totals).astype(jnp.bfloat16)
    context = jnp.einsum(
        "ckgtp,cpkd->ctkgd", past_weights, stored_values, preferred_element_type=jnp.float32
    )
    context = context + jnp.einsum(
        "ckgts,cskd->ctkgd", fresh_weights, fresh_values, preferred_element_type=jnp.float32
    )
    return context.astype(jnp.bfloat16).reshape(span_count * window, kv_local * group * HD)


def a2a_sum(x, axis, dim, count):
    shape = x.shape
    split = shape[:dim] + (count, shape[dim] // count) + shape[dim + 1:]
    received = lax.all_to_all(x.reshape(split), axis, split_axis=dim, concat_axis=dim, tiled=True)
    return jnp.sum(received, axis=dim)


def a2a_gather(x, axis, count):
    spread = jnp.broadcast_to(x[None], (count,) + x.shape)
    return lax.all_to_all(spread, axis, split_axis=0, concat_axis=0, tiled=True)


def doubling_sum(x, axis, count):
    step = 1
    while step < count:
        x = x + lax.ppermute(x, axis, [(a, a ^ step) for a in range(count)])
        step *= 2
    return x


def shards(
    residual,
    queries,
    new_keys,
    new_values,
    cache_keys,
    cache_values,
    out_weight,
    ffn_gain,
    router,
    routes,
    w_gate,
    w_up,
    w_down,
    summary_gain,
    reduce_scale,
    assign,
):
    expert_count = lax.axis_size("expert")
    dp_index = lax.axis_index("dp")
    column = lax.axis_index("expert")
    span_local = cache_keys.shape[0]
    tok_local = residual.shape[0]
    width = residual.shape[1]
    slice_width = width // expert_count
    highest_precision = lax.Precision.HIGHEST
    attended = attend(queries, new_keys, new_values, cache_keys, cache_values)
    n_dp = lax.axis_size("dp")
    weight_blocks = a2a_gather(out_weight, "dp", n_dp)
    head_terms = jnp.einsum(
        "th,shc->tsc", attended, weight_blocks, preferred_element_type=jnp.float32
    ).reshape(attended.shape[0], width)
    mixed = residual.astype(jnp.float32) + a2a_sum(head_terms, "expert", 0, expert_count)
    normed = (
        mixed * lax.rsqrt(jnp.mean(mixed * mixed, axis=-1, keepdims=True) + EPSILON) * ffn_gain
    ).astype(jnp.bfloat16)
    expert_ids = jnp.arange(EXPERTS, dtype=jnp.int32)
    first = routes[:, 0:1] == expert_ids[None, :]
    second = routes[:, 1:2] == expert_ids[None, :]
    partner = jnp.where(first, routes[:, 1:2], jnp.where(second, routes[:, 0:1], -1))
    outgoing = jnp.where((partner >= 0).T[:, :, None], normed[None, :, :], 0)
    arrived_rows, arrived_partner = (
        lax.all_to_all(outgoing, "expert", split_axis=0, concat_axis=1, tiled=True),
        lax.all_to_all(partner.T, "expert", split_axis=0, concat_axis=1, tiled=True),
    )
    present = (arrived_partner >= 0).astype(jnp.int32)
    position = jnp.cumsum(present, axis=1) - 1
    picker = (present[:, None, :] > 0) & (
        position[:, None, :] == jnp.arange(GROUP_CAP)[None, :, None]
    )
    compact = jnp.einsum(
        "eks,esd->ked",
        picker.astype(jnp.bfloat16),
        arrived_rows,
        preferred_element_type=jnp.float32,
    ).astype(jnp.bfloat16)
    arrived_count = arrived_partner.shape[1]
    pick = picker[0]
    slot_present = jnp.any(pick, axis=1)
    slot_partner = jnp.sum(jnp.where(pick, arrived_partner[0][None, :], 0), axis=1)
    local_span = jnp.arange(arrived_count) // WIN
    slot_span = jnp.sum(jnp.where(pick, local_span[None, :], 0), axis=1)
    slot_logits = jnp.dot(compact[:, 0, :], router, preferred_element_type=jnp.float32)
    own_logit = jnp.sum(jnp.where(expert_ids[None, :] == column, slot_logits, 0.0), axis=-1)
    partner_logit = jnp.sum(
        jnp.where(expert_ids[None, :] == slot_partner[:, None], slot_logits, 0.0), axis=-1
    )
    slot_gate = jnp.where(slot_present, jax.nn.sigmoid(own_logit - partner_logit), 0.0)
    pool_weight = jnp.where(
        slot_span[:, None] == jnp.arange(span_local)[None, :], slot_gate[:, None], 0.0
    )
    gathered = a2a_gather(compact, "dp", n_dp).reshape((n_dp * GROUP_CAP,) + compact.shape[1:])
    gathered_weight = a2a_gather(pool_weight, "dp", n_dp)
    gate_proj = jnp.einsum("ned,edf->nf", gathered, w_gate, preferred_element_type=jnp.float32)
    up_proj = jnp.einsum("ned,edf->nf", gathered, w_up, preferred_element_type=jnp.float32)
    hidden = (jax.nn.silu(gate_proj) * up_proj).astype(jnp.bfloat16)
    span_hidden = jnp.einsum(
        "iks,ikf->isf",
        gathered_weight.reshape(n_dp, GROUP_CAP, span_local),
        hidden.reshape(n_dp, GROUP_CAP, -1).astype(jnp.float32),
        precision=highest_precision,
    ).reshape(n_dp * span_local, -1)
    pooled_part = jnp.dot(
        span_hidden, w_down[0].astype(jnp.float32), precision=highest_precision
    )
    own_span = dp_index * span_local + (column * tok_local) // WIN
    span_count = n_dp * span_local
    mixed_sum = jnp.sum(mixed, axis=0)
    pooled_part = pooled_part + jnp.where(
        (jnp.arange(span_count) == own_span)[:, None], mixed_sum[None, :], 0.0
    )
    pooled_cols = a2a_sum(pooled_part, "expert", 1, expert_count)
    pooled_cols = doubling_sum(pooled_cols, "dp", n_dp)
    squares = doubling_sum(jnp.sum(pooled_cols * pooled_cols, axis=-1), "expert", expert_count)
    everyone = (
        pooled_cols * lax.rsqrt(squares / width + EPSILON)[:, None] * summary_gain
    ).astype(jnp.bfloat16)
    summary = lax.dynamic_slice_in_dim(everyone, dp_index * span_local, span_local)
    heads_local = slice_width // HD
    mine = summary.reshape(span_local, heads_local, HD)
    others = everyone.reshape(everyone.shape[0], heads_local, HD)
    factor = reduce_scale / math.sqrt(HD)
    scores = (
        jnp.einsum("chd,khd->hck", mine, others, preferred_element_type=jnp.float32)
        * factor[:, None, None]
    )
    own_assign = lax.dynamic_slice_in_dim(assign, dp_index * span_local, span_local)
    same = own_assign[:, None] == assign[None, :]
    scores = jnp.where(same[None], scores, -jnp.inf)
    highest = jnp.max(scores, axis=-1, keepdims=True)
    expo = jnp.exp(scores - highest)
    weights = (expo / jnp.sum(expo, axis=-1, keepdims=True)).astype(jnp.bfloat16)
    reduced = jnp.einsum("hck,khd->chd", weights, others, preferred_element_type=jnp.float32)
    reduced = reduced.reshape(span_local, slice_width).astype(jnp.bfloat16)
    return (summary, reduced)


def solution(mesh):
    return jax.shard_map(
        shards,
        mesh=mesh,
        in_specs=(
            P(("dp", "expert"), None),
            P("dp", "expert"),
            P("dp", "expert"),
            P("dp", "expert"),
            P("dp", None, "expert"),
            P("dp", None, "expert"),
            P("expert", "dp"),
            P(),
            P(),
            P(("dp", "expert"), None),
            P("expert", None, "dp"),
            P("expert", None, "dp"),
            P("expert", "dp", None),
            P("expert"),
            P("expert"),
            P(),
        ),
        out_specs=(P("dp", "expert"), P("dp", "expert")),
        check_vma=False,
    )
```

```python
import math

import jax
import jax.numpy as jnp
from jax import lax
from jax.sharding import PartitionSpec as P

HEADS = 32
KVH = 8
HD = 128
EXPERTS = 8
WIN = 32
GROUP_CAP = 24


EPSILON = 1e-05
DP = ("z", "y")


def attend(queries, new_keys, new_values, cache_keys, cache_values):
    span_count, cache_len, kv_width = cache_keys.shape
    kv_local = kv_width // HD
    group = HEADS // KVH
    window = queries.shape[0] // span_count
    query_view = queries.reshape(span_count, window, kv_local, group, HD)
    fresh_keys = new_keys.reshape(span_count, window, kv_local, HD)
    fresh_values = new_values.reshape(span_count, window, kv_local, HD)
    stored_keys = cache_keys.reshape(span_count, cache_len, kv_local, HD)
    stored_values = cache_values.reshape(span_count, cache_len, kv_local, HD)
    factor = 1.0 / math.sqrt(HD)
    past_scores = (
        jnp.einsum("ctkgd,cpkd->ckgtp", query_view, stored_keys, preferred_element_type=jnp.float32)
        * factor
    )
    fresh_scores = (
        jnp.einsum("ctkgd,cskd->ckgts", query_view, fresh_keys, preferred_element_type=jnp.float32)
        * factor
    )
    causal = jnp.arange(window)[:, None] >= jnp.arange(window)[None, :]
    fresh_scores = jnp.where(causal, fresh_scores, -jnp.inf)
    highest = jnp.maximum(jnp.max(past_scores, axis=-1), jnp.max(fresh_scores, axis=-1))[..., None]
    past_exp = jnp.exp(past_scores - highest)
    fresh_exp = jnp.exp(fresh_scores - highest)
    totals = jnp.sum(past_exp, axis=-1, keepdims=True) + jnp.sum(fresh_exp, axis=-1, keepdims=True)
    past_weights = (past_exp / totals).astype(jnp.bfloat16)
    fresh_weights = (fresh_exp / totals).astype(jnp.bfloat16)
    context = jnp.einsum(
        "ckgtp,cpkd->ctkgd", past_weights, stored_values, preferred_element_type=jnp.float32
    )
    context = context + jnp.einsum(
        "ckgts,cskd->ctkgd", fresh_weights, fresh_values, preferred_element_type=jnp.float32
    )
    return context.astype(jnp.bfloat16).reshape(span_count * window, kv_local * group * HD)


def a2a_sum(x, axis, dim, count):
    shape = x.shape
    split = shape[:dim] + (count, shape[dim] // count) + shape[dim + 1:]
    received = lax.all_to_all(x.reshape(split), axis, split_axis=dim, concat_axis=dim, tiled=True)
    return jnp.sum(received, axis=dim)


def dp_gather(x, axis):
    return lax.all_gather(lax.all_gather(x, "y", axis=axis, tiled=True), "z", axis=axis, tiled=True)


def doubling_sum(x, axis, count):
    step = 1
    while step < count:
        x = x + lax.ppermute(x, axis, [(a, a ^ step) for a in range(count)])
        step *= 2
    return x


def shards(
    residual,
    queries,
    new_keys,
    new_values,
    cache_keys,
    cache_values,
    out_weight,
    ffn_gain,
    router,
    routes,
    w_gate,
    w_up,
    w_down,
    summary_gain,
    reduce_scale,
    assign,
):
    expert_count = lax.axis_size("expert")
    dp_index = lax.axis_index(DP)
    column = lax.axis_index("expert")
    span_local = cache_keys.shape[0]
    tok_local = residual.shape[0]
    width = residual.shape[1]
    slice_width = width // expert_count
    highest_precision = lax.Precision.HIGHEST
    attended = attend(queries, new_keys, new_values, cache_keys, cache_values)
    head_terms = jnp.dot(
        attended,
        dp_gather(out_weight, 1),
        preferred_element_type=jnp.float32,
    )
    mixed = residual.astype(jnp.float32) + a2a_sum(head_terms, "expert", 0, expert_count)
    normed = (
        mixed * lax.rsqrt(jnp.mean(mixed * mixed, axis=-1, keepdims=True) + EPSILON) * ffn_gain
    ).astype(jnp.bfloat16)
    expert_ids = jnp.arange(EXPERTS, dtype=jnp.int32)
    first = routes[:, 0:1] == expert_ids[None, :]
    second = routes[:, 1:2] == expert_ids[None, :]
    partner = jnp.where(first, routes[:, 1:2], jnp.where(second, routes[:, 0:1], -1))
    outgoing = jnp.where((partner >= 0).T[:, :, None], normed[None, :, :], 0)
    arrived_rows, arrived_partner = (
        lax.all_to_all(outgoing, "expert", split_axis=0, concat_axis=1, tiled=True),
        lax.all_to_all(partner.T, "expert", split_axis=0, concat_axis=1, tiled=True),
    )
    present = (arrived_partner >= 0).astype(jnp.int32)
    position = jnp.cumsum(present, axis=1) - 1
    picker = (present[:, None, :] > 0) & (
        position[:, None, :] == jnp.arange(GROUP_CAP)[None, :, None]
    )
    compact = jnp.einsum(
        "eks,esd->ked",
        picker.astype(jnp.bfloat16),
        arrived_rows,
        preferred_element_type=jnp.float32,
    ).astype(jnp.bfloat16)
    arrived_count = arrived_partner.shape[1]
    pick = picker[0]
    slot_present = jnp.any(pick, axis=1)
    slot_partner = jnp.sum(jnp.where(pick, arrived_partner[0][None, :], 0), axis=1)
    local_span = jnp.arange(arrived_count) // WIN
    slot_span = jnp.sum(jnp.where(pick, local_span[None, :], 0), axis=1)
    slot_logits = jnp.dot(compact[:, 0, :], router, preferred_element_type=jnp.float32)
    own_logit = jnp.sum(jnp.where(expert_ids[None, :] == column, slot_logits, 0.0), axis=-1)
    partner_logit = jnp.sum(
        jnp.where(expert_ids[None, :] == slot_partner[:, None], slot_logits, 0.0), axis=-1
    )
    slot_gate = jnp.where(slot_present, jax.nn.sigmoid(own_logit - partner_logit), 0.0)
    pool_weight = jnp.where(
        slot_span[:, None] == jnp.arange(span_local)[None, :], slot_gate[:, None], 0.0
    )
    gathered = dp_gather(compact, 0)
    gathered_weight = lax.all_gather(pool_weight, DP, axis=0, tiled=True)
    n_dp = gathered.shape[0] // GROUP_CAP
    gate_proj = jnp.einsum("ned,edf->nf", gathered, w_gate, preferred_element_type=jnp.float32)
    up_proj = jnp.einsum("ned,edf->nf", gathered, w_up, preferred_element_type=jnp.float32)
    hidden = (jax.nn.silu(gate_proj) * up_proj).astype(jnp.bfloat16)
    span_hidden = jnp.einsum(
        "iks,ikf->isf",
        gathered_weight.reshape(n_dp, GROUP_CAP, span_local),
        hidden.reshape(n_dp, GROUP_CAP, -1).astype(jnp.float32),
        precision=highest_precision,
    ).reshape(n_dp * span_local, -1)
    pooled_part = jnp.dot(
        span_hidden, w_down[0].astype(jnp.float32), precision=highest_precision
    )
    own_span = dp_index * span_local + (column * tok_local) // WIN
    span_count = n_dp * span_local
    mixed_sum = jnp.sum(mixed, axis=0)
    pooled_part = pooled_part + jnp.where(
        (jnp.arange(span_count) == own_span)[:, None], mixed_sum[None, :], 0.0
    )
    pooled_cols = a2a_sum(pooled_part, "expert", 1, expert_count)
    pooled_cols = doubling_sum(pooled_cols, DP, n_dp)
    squares = doubling_sum(jnp.sum(pooled_cols * pooled_cols, axis=-1), "expert", expert_count)
    everyone = (
        pooled_cols * lax.rsqrt(squares / width + EPSILON)[:, None] * summary_gain
    ).astype(jnp.bfloat16)
    summary = lax.dynamic_slice_in_dim(everyone, dp_index * span_local, span_local)
    heads_local = slice_width // HD
    mine = summary.reshape(span_local, heads_local, HD)
    others = everyone.reshape(everyone.shape[0], heads_local, HD)
    factor = reduce_scale / math.sqrt(HD)
    scores = (
        jnp.einsum("chd,khd->hck", mine, others, preferred_element_type=jnp.float32)
        * factor[:, None, None]
    )
    own_assign = lax.dynamic_slice_in_dim(assign, dp_index * span_local, span_local)
    same = own_assign[:, None] == assign[None, :]
    scores = jnp.where(same[None], scores, -jnp.inf)
    highest = jnp.max(scores, axis=-1, keepdims=True)
    expo = jnp.exp(scores - highest)
    weights = (expo / jnp.sum(expo, axis=-1, keepdims=True)).astype(jnp.bfloat16)
    reduced = jnp.einsum("hck,khd->chd", weights, others, preferred_element_type=jnp.float32)
    reduced = reduced.reshape(span_local, slice_width).astype(jnp.bfloat16)
    return (summary, reduced)


def solution(mesh):
    dp_size, expert_size = mesh.devices.shape
    y_size = 4
    split_mesh = jax.sharding.Mesh(
        mesh.devices.reshape(dp_size // y_size, y_size, expert_size), ("z", "y", "expert")
    )
    return jax.shard_map(
        shards,
        mesh=split_mesh,
        in_specs=(
            P((*DP, "expert"), None),
            P(DP, "expert"),
            P(DP, "expert"),
            P(DP, "expert"),
            P(DP, None, "expert"),
            P(DP, None, "expert"),
            P("expert", DP),
            P(),
            P(),
            P((*DP, "expert"), None),
            P("expert", None, DP),
            P("expert", None, DP),
            P("expert", DP, None),
            P("expert"),
            P("expert"),
            P(),
        ),
        out_specs=(P(DP, "expert"), P(DP, "expert")),
        check_vma=False,
    )
```

```python
import math

import jax
import jax.numpy as jnp
from jax import lax
from jax.sharding import PartitionSpec as P

HEADS = 32
KVH = 8
HD = 128
EXPERTS = 8
WIN = 32
GROUP_CAP = 24


EPSILON = 1e-05
DP = ("z", "y")


def attend(queries, new_keys, new_values, cache_keys, cache_values):
    span_count, cache_len, kv_width = cache_keys.shape
    kv_local = kv_width // HD
    group = HEADS // KVH
    window = queries.shape[0] // span_count
    query_view = queries.reshape(span_count, window, kv_local, group, HD)
    fresh_keys = new_keys.reshape(span_count, window, kv_local, HD)
    fresh_values = new_values.reshape(span_count, window, kv_local, HD)
    stored_keys = cache_keys.reshape(span_count, cache_len, kv_local, HD)
    stored_values = cache_values.reshape(span_count, cache_len, kv_local, HD)
    factor = 1.0 / math.sqrt(HD)
    past_scores = (
        jnp.einsum("ctkgd,cpkd->ckgtp", query_view, stored_keys, preferred_element_type=jnp.float32)
        * factor
    )
    fresh_scores = (
        jnp.einsum("ctkgd,cskd->ckgts", query_view, fresh_keys, preferred_element_type=jnp.float32)
        * factor
    )
    causal = jnp.arange(window)[:, None] >= jnp.arange(window)[None, :]
    fresh_scores = jnp.where(causal, fresh_scores, -jnp.inf)
    highest = jnp.maximum(jnp.max(past_scores, axis=-1), jnp.max(fresh_scores, axis=-1))[..., None]
    past_exp = jnp.exp(past_scores - highest)
    fresh_exp = jnp.exp(fresh_scores - highest)
    totals = jnp.sum(past_exp, axis=-1, keepdims=True) + jnp.sum(fresh_exp, axis=-1, keepdims=True)
    past_weights = (past_exp / totals).astype(jnp.bfloat16)
    fresh_weights = (fresh_exp / totals).astype(jnp.bfloat16)
    context = jnp.einsum(
        "ckgtp,cpkd->ctkgd", past_weights, stored_values, preferred_element_type=jnp.float32
    )
    context = context + jnp.einsum(
        "ckgts,cskd->ctkgd", fresh_weights, fresh_values, preferred_element_type=jnp.float32
    )
    return context.astype(jnp.bfloat16).reshape(span_count * window, kv_local * group * HD)


def a2a_sum(x, axis, dim, count):
    shape = x.shape
    split = shape[:dim] + (count, shape[dim] // count) + shape[dim + 1:]
    received = lax.all_to_all(x.reshape(split), axis, split_axis=dim, concat_axis=dim, tiled=True)
    return jnp.sum(received, axis=dim)


def a2a_gather(x, axis, count):
    spread = jnp.broadcast_to(x[None], (count,) + x.shape)
    return lax.all_to_all(spread, axis, split_axis=0, concat_axis=0, tiled=True)


def dp_gather(x, axis):
    return lax.all_gather(lax.all_gather(x, "y", axis=axis, tiled=True), "z", axis=axis, tiled=True)


def doubling_sum(x, axis, count):
    step = 1
    while step < count:
        x = x + lax.ppermute(x, axis, [(a, a ^ step) for a in range(count)])
        step *= 2
    return x


def shards(
    residual,
    queries,
    new_keys,
    new_values,
    cache_keys,
    cache_values,
    out_weight,
    ffn_gain,
    router,
    routes,
    w_gate,
    w_up,
    w_down,
    summary_gain,
    reduce_scale,
    assign,
):
    expert_count = lax.axis_size("expert")
    dp_index = lax.axis_index(DP)
    column = lax.axis_index("expert")
    span_local = cache_keys.shape[0]
    tok_local = residual.shape[0]
    width = residual.shape[1]
    slice_width = width // expert_count
    highest_precision = lax.Precision.HIGHEST
    attended = attend(queries, new_keys, new_values, cache_keys, cache_values)
    head_terms = jnp.dot(
        attended,
        dp_gather(out_weight, 1),
        preferred_element_type=jnp.float32,
    )
    mixed = residual.astype(jnp.float32) + a2a_sum(head_terms, "expert", 0, expert_count)
    normed = (
        mixed * lax.rsqrt(jnp.mean(mixed * mixed, axis=-1, keepdims=True) + EPSILON) * ffn_gain
    ).astype(jnp.bfloat16)
    expert_ids = jnp.arange(EXPERTS, dtype=jnp.int32)
    first = routes[:, 0:1] == expert_ids[None, :]
    second = routes[:, 1:2] == expert_ids[None, :]
    partner = jnp.where(first, routes[:, 1:2], jnp.where(second, routes[:, 0:1], -1))
    tag_width = 128
    tag = jnp.broadcast_to(((partner + 1).T)[:, :, None], partner.T.shape + (tag_width,))
    outgoing = jnp.concatenate(
        [jnp.where((partner >= 0).T[:, :, None], normed[None, :, :], 0), tag.astype(jnp.bfloat16)],
        axis=2,
    )
    arrived = lax.all_to_all(outgoing, "expert", split_axis=0, concat_axis=1, tiled=True)
    arrived_rows = arrived[:, :, :width]
    arrived_partner = arrived[:, :, width].astype(jnp.int32) - 1
    present = (arrived_partner >= 0).astype(jnp.int32)
    position = jnp.cumsum(present, axis=1) - 1
    picker = (present[:, None, :] > 0) & (
        position[:, None, :] == jnp.arange(GROUP_CAP)[None, :, None]
    )
    compact = jnp.einsum(
        "eks,esd->ked",
        picker.astype(jnp.bfloat16),
        arrived_rows,
        preferred_element_type=jnp.float32,
    ).astype(jnp.bfloat16)
    arrived_count = arrived_partner.shape[1]
    pick = picker[0]
    slot_present = jnp.any(pick, axis=1)
    slot_partner = jnp.sum(jnp.where(pick, arrived_partner[0][None, :], 0), axis=1)
    local_span = jnp.arange(arrived_count) // WIN
    slot_span = jnp.sum(jnp.where(pick, local_span[None, :], 0), axis=1)
    slot_logits = jnp.dot(compact[:, 0, :], router, preferred_element_type=jnp.float32)
    own_logit = jnp.sum(jnp.where(expert_ids[None, :] == column, slot_logits, 0.0), axis=-1)
    partner_logit = jnp.sum(
        jnp.where(expert_ids[None, :] == slot_partner[:, None], slot_logits, 0.0), axis=-1
    )
    slot_gate = jnp.where(slot_present, jax.nn.sigmoid(own_logit - partner_logit), 0.0)
    pool_weight = jnp.where(
        slot_span[:, None] == jnp.arange(span_local)[None, :], slot_gate[:, None], 0.0
    )
    gathered = dp_gather(compact, 0)
    gathered_weight = lax.all_gather(pool_weight, DP, axis=0, tiled=True)
    n_dp = gathered.shape[0] // GROUP_CAP
    gate_proj = jnp.einsum("ned,edf->nf", gathered, w_gate, preferred_element_type=jnp.float32)
    up_proj = jnp.einsum("ned,edf->nf", gathered, w_up, preferred_element_type=jnp.float32)
    hidden = (jax.nn.silu(gate_proj) * up_proj).astype(jnp.bfloat16)
    span_hidden = jnp.einsum(
        "iks,ikf->isf",
        gathered_weight.reshape(n_dp, GROUP_CAP, span_local),
        hidden.reshape(n_dp, GROUP_CAP, -1).astype(jnp.float32),
        precision=highest_precision,
    ).reshape(n_dp * span_local, -1)
    pooled_part = jnp.dot(
        span_hidden, w_down[0].astype(jnp.float32), precision=highest_precision
    )
    own_span = dp_index * span_local + (column * tok_local) // WIN
    span_count = n_dp * span_local
    mixed_sum = jnp.sum(mixed, axis=0)
    pooled_part = pooled_part + jnp.where(
        (jnp.arange(span_count) == own_span)[:, None], mixed_sum[None, :], 0.0
    )
    pooled_cols = a2a_sum(pooled_part, "expert", 1, expert_count)
    own_cols = a2a_sum(pooled_cols, DP, 0, n_dp)
    squares = doubling_sum(jnp.sum(own_cols * own_cols, axis=-1), "expert", expert_count)
    summary = (
        own_cols * lax.rsqrt(squares / width + EPSILON)[:, None] * summary_gain
    ).astype(jnp.bfloat16)
    everyone = a2a_gather(summary, DP, n_dp).reshape(n_dp * span_local, slice_width)
    heads_local = slice_width // HD
    mine = summary.reshape(span_local, heads_local, HD)
    others = everyone.reshape(everyone.shape[0], heads_local, HD)
    factor = reduce_scale / math.sqrt(HD)
    scores = (
        jnp.einsum("chd,khd->hck", mine, others, preferred_element_type=jnp.float32)
        * factor[:, None, None]
    )
    own_assign = lax.dynamic_slice_in_dim(assign, dp_index * span_local, span_local)
    same = own_assign[:, None] == assign[None, :]
    scores = jnp.where(same[None], scores, -jnp.inf)
    highest = jnp.max(scores, axis=-1, keepdims=True)
    expo = jnp.exp(scores - highest)
    weights = (expo / jnp.sum(expo, axis=-1, keepdims=True)).astype(jnp.bfloat16)
    reduced = jnp.einsum("hck,khd->chd", weights, others, preferred_element_type=jnp.float32)
    reduced = reduced.reshape(span_local, slice_width).astype(jnp.bfloat16)
    return (summary, reduced)


def solution(mesh):
    dp_size, expert_size = mesh.devices.shape
    y_size = 4
    split_mesh = jax.sharding.Mesh(
        mesh.devices.reshape(dp_size // y_size, y_size, expert_size), ("z", "y", "expert")
    )
    return jax.shard_map(
        shards,
        mesh=split_mesh,
        in_specs=(
            P((*DP, "expert"), None),
            P(DP, "expert"),
            P(DP, "expert"),
            P(DP, "expert"),
            P(DP, None, "expert"),
            P(DP, None, "expert"),
            P("expert", DP),
            P(),
            P(),
            P((*DP, "expert"), None),
            P("expert", None, DP),
            P("expert", None, DP),
            P("expert", DP, None),
            P("expert"),
            P("expert"),
            P(),
        ),
        out_specs=(P(DP, "expert"), P(DP, "expert")),
        check_vma=False,
    )
```

```python
import math

import jax
import jax.numpy as jnp
from jax import lax
from jax.sharding import PartitionSpec as P

HEADS = 32
KVH = 8
HD = 128
EXPERTS = 8
WIN = 32
GROUP_CAP = 24


EPSILON = 1e-05
DP = ("z", "y")


def attend(queries, new_keys, new_values, cache_keys, cache_values):
    span_count, cache_len, kv_width = cache_keys.shape
    kv_local = kv_width // HD
    group = HEADS // KVH
    window = queries.shape[0] // span_count
    query_view = queries.reshape(span_count, window, kv_local, group, HD)
    fresh_keys = new_keys.reshape(span_count, window, kv_local, HD)
    fresh_values = new_values.reshape(span_count, window, kv_local, HD)
    stored_keys = cache_keys.reshape(span_count, cache_len, kv_local, HD)
    stored_values = cache_values.reshape(span_count, cache_len, kv_local, HD)
    factor = 1.0 / math.sqrt(HD)
    past_scores = (
        jnp.einsum("ctkgd,cpkd->ckgtp", query_view, stored_keys, preferred_element_type=jnp.float32)
        * factor
    )
    fresh_scores = (
        jnp.einsum("ctkgd,cskd->ckgts", query_view, fresh_keys, preferred_element_type=jnp.float32)
        * factor
    )
    causal = jnp.arange(window)[:, None] >= jnp.arange(window)[None, :]
    fresh_scores = jnp.where(causal, fresh_scores, -jnp.inf)
    highest = jnp.maximum(jnp.max(past_scores, axis=-1), jnp.max(fresh_scores, axis=-1))[..., None]
    past_exp = jnp.exp(past_scores - highest)
    fresh_exp = jnp.exp(fresh_scores - highest)
    totals = jnp.sum(past_exp, axis=-1, keepdims=True) + jnp.sum(fresh_exp, axis=-1, keepdims=True)
    past_weights = (past_exp / totals).astype(jnp.bfloat16)
    fresh_weights = (fresh_exp / totals).astype(jnp.bfloat16)
    context = jnp.einsum(
        "ckgtp,cpkd->ctkgd", past_weights, stored_values, preferred_element_type=jnp.float32
    )
    context = context + jnp.einsum(
        "ckgts,cskd->ctkgd", fresh_weights, fresh_values, preferred_element_type=jnp.float32
    )
    return context.astype(jnp.bfloat16).reshape(span_count * window, kv_local * group * HD)


def a2a_sum(x, axis, dim, count):
    shape = x.shape
    split = shape[:dim] + (count, shape[dim] // count) + shape[dim + 1:]
    received = lax.all_to_all(x.reshape(split), axis, split_axis=dim, concat_axis=dim, tiled=True)
    return jnp.sum(received, axis=dim)


def a2a_gather(x, axis, count):
    spread = jnp.broadcast_to(x[None], (count,) + x.shape)
    return lax.all_to_all(spread, axis, split_axis=0, concat_axis=0, tiled=True)


def dp_gather(x, axis):
    return lax.all_gather(lax.all_gather(x, "y", axis=axis, tiled=True), "z", axis=axis, tiled=True)


def doubling_sum(x, axis, count):
    step = 1
    while step < count:
        x = x + lax.ppermute(x, axis, [(a, a ^ step) for a in range(count)])
        step *= 2
    return x


def shards(
    residual,
    queries,
    new_keys,
    new_values,
    cache_keys,
    cache_values,
    out_weight,
    ffn_gain,
    router,
    routes,
    w_gate,
    w_up,
    w_down,
    summary_gain,
    reduce_scale,
    assign,
):
    expert_count = lax.axis_size("expert")
    dp_index = lax.axis_index(DP)
    column = lax.axis_index("expert")
    span_local = cache_keys.shape[0]
    tok_local = residual.shape[0]
    width = residual.shape[1]
    slice_width = width // expert_count
    highest_precision = lax.Precision.HIGHEST
    attended = attend(queries, new_keys, new_values, cache_keys, cache_values)
    y_count = lax.axis_size("y")
    z_count = lax.axis_size("z")
    attended_row = lax.all_gather(attended, "y", axis=0, tiled=True)
    weight_row = lax.all_gather(out_weight, "z", axis=1, tiled=True)
    col_block = out_weight.shape[1]
    head_terms = jnp.dot(attended_row, weight_row, preferred_element_type=jnp.float32)
    head_terms = head_terms.reshape(y_count, expert_count, tok_local, z_count * col_block)
    head_terms = head_terms.transpose(1, 0, 2, 3)
    token_cols = a2a_sum(head_terms, "expert", 0, expert_count)[0]
    token_cols = lax.all_to_all(token_cols, "y", split_axis=0, concat_axis=0, tiled=True)
    token_cols = token_cols.reshape(y_count, tok_local, z_count, col_block).transpose(1, 2, 0, 3)
    mixed = residual.astype(jnp.float32) + token_cols.reshape(tok_local, width)
    normed = (
        mixed * lax.rsqrt(jnp.mean(mixed * mixed, axis=-1, keepdims=True) + EPSILON) * ffn_gain
    ).astype(jnp.bfloat16)
    expert_ids = jnp.arange(EXPERTS, dtype=jnp.int32)
    first = routes[:, 0:1] == expert_ids[None, :]
    second = routes[:, 1:2] == expert_ids[None, :]
    partner = jnp.where(first, routes[:, 1:2], jnp.where(second, routes[:, 0:1], -1))
    tag_width = 128
    tag = jnp.broadcast_to(((partner + 1).T)[:, :, None], partner.T.shape + (tag_width,))
    outgoing = jnp.concatenate(
        [jnp.where((partner >= 0).T[:, :, None], normed[None, :, :], 0), tag.astype(jnp.bfloat16)],
        axis=2,
    )
    arrived = lax.all_to_all(outgoing, "expert", split_axis=0, concat_axis=1, tiled=True)
    arrived_rows = arrived[:, :, :width]
    arrived_partner = arrived[:, :, width].astype(jnp.int32) - 1
    present = (arrived_partner >= 0).astype(jnp.int32)
    position = jnp.cumsum(present, axis=1) - 1
    picker = (present[:, None, :] > 0) & (
        position[:, None, :] == jnp.arange(GROUP_CAP)[None, :, None]
    )
    compact = jnp.einsum(
        "eks,esd->ked",
        picker.astype(jnp.bfloat16),
        arrived_rows,
        preferred_element_type=jnp.float32,
    ).astype(jnp.bfloat16)
    arrived_count = arrived_partner.shape[1]
    pick = picker[0]
    slot_present = jnp.any(pick, axis=1)
    slot_partner = jnp.sum(jnp.where(pick, arrived_partner[0][None, :], 0), axis=1)
    local_span = jnp.arange(arrived_count) // WIN
    slot_span = jnp.sum(jnp.where(pick, local_span[None, :], 0), axis=1)
    slot_logits = jnp.dot(compact[:, 0, :], router, preferred_element_type=jnp.float32)
    own_logit = jnp.sum(jnp.where(expert_ids[None, :] == column, slot_logits, 0.0), axis=-1)
    partner_logit = jnp.sum(
        jnp.where(expert_ids[None, :] == slot_partner[:, None], slot_logits, 0.0), axis=-1
    )
    slot_gate = jnp.where(slot_present, jax.nn.sigmoid(own_logit - partner_logit), 0.0)
    pool_weight = jnp.where(
        slot_span[:, None] == jnp.arange(span_local)[None, :], slot_gate[:, None], 0.0
    )
    gathered = dp_gather(compact, 0)
    gathered_weight = lax.all_gather(pool_weight, DP, axis=0, tiled=True)
    n_dp = gathered.shape[0] // GROUP_CAP
    gate_proj = jnp.einsum("ned,edf->nf", gathered, w_gate, preferred_element_type=jnp.float32)
    up_proj = jnp.einsum("ned,edf->nf", gathered, w_up, preferred_element_type=jnp.float32)
    hidden = (jax.nn.silu(gate_proj) * up_proj).astype(jnp.bfloat16)
    span_hidden = jnp.einsum(
        "iks,ikf->isf",
        gathered_weight.reshape(n_dp, GROUP_CAP, span_local),
        hidden.reshape(n_dp, GROUP_CAP, -1).astype(jnp.float32),
        precision=highest_precision,
    ).reshape(n_dp * span_local, -1)
    pooled_part = jnp.dot(
        span_hidden, w_down[0].astype(jnp.float32), precision=highest_precision
    )
    own_span = dp_index * span_local + (column * tok_local) // WIN
    span_count = n_dp * span_local
    mixed_sum = jnp.sum(mixed, axis=0)
    pooled_part = pooled_part + jnp.where(
        (jnp.arange(span_count) == own_span)[:, None], mixed_sum[None, :], 0.0
    )
    pooled_cols = a2a_sum(pooled_part, "expert", 1, expert_count)
    own_cols = a2a_sum(pooled_cols, DP, 0, n_dp)
    squares = doubling_sum(jnp.sum(own_cols * own_cols, axis=-1), "expert", expert_count)
    summary = (
        own_cols * lax.rsqrt(squares / width + EPSILON)[:, None] * summary_gain
    ).astype(jnp.bfloat16)
    everyone = a2a_gather(summary, DP, n_dp).reshape(n_dp * span_local, slice_width)
    heads_local = slice_width // HD
    mine = summary.reshape(span_local, heads_local, HD)
    others = everyone.reshape(everyone.shape[0], heads_local, HD)
    factor = reduce_scale / math.sqrt(HD)
    scores = (
        jnp.einsum("chd,khd->hck", mine, others, preferred_element_type=jnp.float32)
        * factor[:, None, None]
    )
    own_assign = lax.dynamic_slice_in_dim(assign, dp_index * span_local, span_local)
    same = own_assign[:, None] == assign[None, :]
    scores = jnp.where(same[None], scores, -jnp.inf)
    highest = jnp.max(scores, axis=-1, keepdims=True)
    expo = jnp.exp(scores - highest)
    weights = (expo / jnp.sum(expo, axis=-1, keepdims=True)).astype(jnp.bfloat16)
    reduced = jnp.einsum("hck,khd->chd", weights, others, preferred_element_type=jnp.float32)
    reduced = reduced.reshape(span_local, slice_width).astype(jnp.bfloat16)
    return (summary, reduced)


def solution(mesh):
    dp_size, expert_size = mesh.devices.shape
    y_size = 4
    split_mesh = jax.sharding.Mesh(
        mesh.devices.reshape(dp_size // y_size, y_size, expert_size), ("z", "y", "expert")
    )
    return jax.shard_map(
        shards,
        mesh=split_mesh,
        in_specs=(
            P((*DP, "expert"), None),
            P(DP, "expert"),
            P(DP, "expert"),
            P(DP, "expert"),
            P(DP, None, "expert"),
            P(DP, None, "expert"),
            P("expert", DP),
            P(),
            P(),
            P((*DP, "expert"), None),
            P("expert", None, DP),
            P("expert", None, DP),
            P("expert", DP, None),
            P("expert"),
            P("expert"),
            P(),
        ),
        out_specs=(P(DP, "expert"), P(DP, "expert")),
        check_vma=False,
    )
```

```python
import math

import jax
import jax.numpy as jnp
from jax import lax
from jax.sharding import PartitionSpec as P

HEADS = 32
KVH = 8
HD = 128
EXPERTS = 8
WIN = 32
GROUP_CAP = 24


EPSILON = 1e-05
DP = ("z", "y")


def attend(queries, new_keys, new_values, cache_keys, cache_values):
    span_count, cache_len, kv_width = cache_keys.shape
    kv_local = kv_width // HD
    group = HEADS // KVH
    window = queries.shape[0] // span_count
    query_view = queries.reshape(span_count, window, kv_local, group, HD)
    fresh_keys = new_keys.reshape(span_count, window, kv_local, HD)
    fresh_values = new_values.reshape(span_count, window, kv_local, HD)
    stored_keys = cache_keys.reshape(span_count, cache_len, kv_local, HD)
    stored_values = cache_values.reshape(span_count, cache_len, kv_local, HD)
    factor = 1.0 / math.sqrt(HD)
    past_scores = (
        jnp.einsum("ctkgd,cpkd->ckgtp", query_view, stored_keys, preferred_element_type=jnp.float32)
        * factor
    )
    fresh_scores = (
        jnp.einsum("ctkgd,cskd->ckgts", query_view, fresh_keys, preferred_element_type=jnp.float32)
        * factor
    )
    causal = jnp.arange(window)[:, None] >= jnp.arange(window)[None, :]
    fresh_scores = jnp.where(causal, fresh_scores, -jnp.inf)
    highest = jnp.maximum(jnp.max(past_scores, axis=-1), jnp.max(fresh_scores, axis=-1))[..., None]
    past_exp = jnp.exp(past_scores - highest)
    fresh_exp = jnp.exp(fresh_scores - highest)
    totals = jnp.sum(past_exp, axis=-1, keepdims=True) + jnp.sum(fresh_exp, axis=-1, keepdims=True)
    past_weights = (past_exp / totals).astype(jnp.bfloat16)
    fresh_weights = (fresh_exp / totals).astype(jnp.bfloat16)
    context = jnp.einsum(
        "ckgtp,cpkd->ctkgd", past_weights, stored_values, preferred_element_type=jnp.float32
    )
    context = context + jnp.einsum(
        "ckgts,cskd->ctkgd", fresh_weights, fresh_values, preferred_element_type=jnp.float32
    )
    return context.astype(jnp.bfloat16).reshape(span_count * window, kv_local * group * HD)


def a2a_sum(x, axis, dim, count):
    shape = x.shape
    split = shape[:dim] + (count, shape[dim] // count) + shape[dim + 1:]
    received = lax.all_to_all(x.reshape(split), axis, split_axis=dim, concat_axis=dim, tiled=True)
    return jnp.sum(received, axis=dim)


def a2a_gather(x, axis, count):
    spread = jnp.broadcast_to(x[None], (count,) + x.shape)
    return lax.all_to_all(spread, axis, split_axis=0, concat_axis=0, tiled=True)


def dp_gather(x, axis):
    return lax.all_gather(lax.all_gather(x, "y", axis=axis, tiled=True), "z", axis=axis, tiled=True)


def doubling_sum(x, axis, count):
    step = 1
    while step < count:
        x = x + lax.ppermute(x, axis, [(a, a ^ step) for a in range(count)])
        step *= 2
    return x


def shards(
    residual,
    queries,
    new_keys,
    new_values,
    cache_keys,
    cache_values,
    out_weight,
    ffn_gain,
    router,
    routes,
    w_gate,
    w_up,
    w_down,
    summary_gain,
    reduce_scale,
    assign,
):
    expert_count = lax.axis_size("expert")
    dp_index = lax.axis_index(DP)
    column = lax.axis_index("expert")
    span_local = cache_keys.shape[0]
    tok_local = residual.shape[0]
    width = residual.shape[1]
    slice_width = width // expert_count
    highest_precision = lax.Precision.HIGHEST
    attended = attend(queries, new_keys, new_values, cache_keys, cache_values)
    y_count = lax.axis_size("y")
    z_count = lax.axis_size("z")
    attended_row = lax.all_gather(attended, "y", axis=0, tiled=True)
    weight_row = a2a_gather(out_weight, "z", z_count)
    col_block = out_weight.shape[1]
    head_terms = jnp.einsum(
        "th,zhc->tzc", attended_row, weight_row, preferred_element_type=jnp.float32
    )
    head_terms = head_terms.reshape(y_count, expert_count, tok_local, z_count * col_block)
    head_terms = head_terms.transpose(1, 0, 2, 3)
    token_cols = a2a_sum(head_terms, "expert", 0, expert_count)[0]
    token_cols = lax.all_to_all(token_cols, "y", split_axis=0, concat_axis=0, tiled=True)
    token_cols = token_cols.reshape(y_count, tok_local, z_count, col_block).transpose(1, 2, 0, 3)
    mixed = residual.astype(jnp.float32) + token_cols.reshape(tok_local, width)
    normed = (
        mixed * lax.rsqrt(jnp.mean(mixed * mixed, axis=-1, keepdims=True) + EPSILON) * ffn_gain
    ).astype(jnp.bfloat16)
    expert_ids = jnp.arange(EXPERTS, dtype=jnp.int32)
    first = routes[:, 0:1] == expert_ids[None, :]
    second = routes[:, 1:2] == expert_ids[None, :]
    partner = jnp.where(first, routes[:, 1:2], jnp.where(second, routes[:, 0:1], -1))
    tag_width = 128
    tag = jnp.broadcast_to(((partner + 1).T)[:, :, None], partner.T.shape + (tag_width,))
    outgoing = jnp.concatenate(
        [jnp.where((partner >= 0).T[:, :, None], normed[None, :, :], 0), tag.astype(jnp.bfloat16)],
        axis=2,
    )
    arrived = lax.all_to_all(outgoing, "expert", split_axis=0, concat_axis=1, tiled=True)
    arrived_rows = arrived[:, :, :width]
    arrived_partner = arrived[:, :, width].astype(jnp.int32) - 1
    present = (arrived_partner >= 0).astype(jnp.int32)
    position = jnp.cumsum(present, axis=1) - 1
    picker = (present[:, None, :] > 0) & (
        position[:, None, :] == jnp.arange(GROUP_CAP)[None, :, None]
    )
    compact = jnp.einsum(
        "eks,esd->ked",
        picker.astype(jnp.bfloat16),
        arrived_rows,
        preferred_element_type=jnp.float32,
    ).astype(jnp.bfloat16)
    arrived_count = arrived_partner.shape[1]
    pick = picker[0]
    slot_present = jnp.any(pick, axis=1)
    slot_partner = jnp.sum(jnp.where(pick, arrived_partner[0][None, :], 0), axis=1)
    local_span = jnp.arange(arrived_count) // WIN
    slot_span = jnp.sum(jnp.where(pick, local_span[None, :], 0), axis=1)
    slot_logits = jnp.dot(compact[:, 0, :], router, preferred_element_type=jnp.float32)
    own_logit = jnp.sum(jnp.where(expert_ids[None, :] == column, slot_logits, 0.0), axis=-1)
    partner_logit = jnp.sum(
        jnp.where(expert_ids[None, :] == slot_partner[:, None], slot_logits, 0.0), axis=-1
    )
    slot_gate = jnp.where(slot_present, jax.nn.sigmoid(own_logit - partner_logit), 0.0)
    pool_weight = jnp.where(
        slot_span[:, None] == jnp.arange(span_local)[None, :], slot_gate[:, None], 0.0
    )
    gathered = dp_gather(compact, 0)
    gathered_weight = lax.all_gather(pool_weight, DP, axis=0, tiled=True)
    n_dp = gathered.shape[0] // GROUP_CAP
    gate_proj = jnp.einsum("ned,edf->nf", gathered, w_gate, preferred_element_type=jnp.float32)
    up_proj = jnp.einsum("ned,edf->nf", gathered, w_up, preferred_element_type=jnp.float32)
    hidden = (jax.nn.silu(gate_proj) * up_proj).astype(jnp.bfloat16)
    span_hidden = jnp.einsum(
        "iks,ikf->isf",
        gathered_weight.reshape(n_dp, GROUP_CAP, span_local),
        hidden.reshape(n_dp, GROUP_CAP, -1).astype(jnp.float32),
        precision=highest_precision,
    ).reshape(n_dp * span_local, -1)
    pooled_part = jnp.dot(
        span_hidden, w_down[0].astype(jnp.float32), precision=highest_precision
    )
    own_span = dp_index * span_local + (column * tok_local) // WIN
    span_count = n_dp * span_local
    mixed_sum = jnp.sum(mixed, axis=0)
    pooled_part = pooled_part + jnp.where(
        (jnp.arange(span_count) == own_span)[:, None], mixed_sum[None, :], 0.0
    )
    pooled_cols = a2a_sum(pooled_part, "expert", 1, expert_count)
    own_cols = a2a_sum(pooled_cols, DP, 0, n_dp)
    squares = doubling_sum(jnp.sum(own_cols * own_cols, axis=-1), "expert", expert_count)
    summary = (
        own_cols * lax.rsqrt(squares / width + EPSILON)[:, None] * summary_gain
    ).astype(jnp.bfloat16)
    everyone = a2a_gather(summary, DP, n_dp).reshape(n_dp * span_local, slice_width)
    heads_local = slice_width // HD
    mine = summary.reshape(span_local, heads_local, HD)
    others = everyone.reshape(everyone.shape[0], heads_local, HD)
    factor = reduce_scale / math.sqrt(HD)
    scores = (
        jnp.einsum("chd,khd->hck", mine, others, preferred_element_type=jnp.float32)
        * factor[:, None, None]
    )
    own_assign = lax.dynamic_slice_in_dim(assign, dp_index * span_local, span_local)
    same = own_assign[:, None] == assign[None, :]
    scores = jnp.where(same[None], scores, -jnp.inf)
    highest = jnp.max(scores, axis=-1, keepdims=True)
    expo = jnp.exp(scores - highest)
    weights = (expo / jnp.sum(expo, axis=-1, keepdims=True)).astype(jnp.bfloat16)
    reduced = jnp.einsum("hck,khd->chd", weights, others, preferred_element_type=jnp.float32)
    reduced = reduced.reshape(span_local, slice_width).astype(jnp.bfloat16)
    return (summary, reduced)


def solution(mesh):
    dp_size, expert_size = mesh.devices.shape
    y_size = 4
    split_mesh = jax.sharding.Mesh(
        mesh.devices.reshape(dp_size // y_size, y_size, expert_size), ("z", "y", "expert")
    )
    return jax.shard_map(
        shards,
        mesh=split_mesh,
        in_specs=(
            P((*DP, "expert"), None),
            P(DP, "expert"),
            P(DP, "expert"),
            P(DP, "expert"),
            P(DP, None, "expert"),
            P(DP, None, "expert"),
            P("expert", DP),
            P(),
            P(),
            P((*DP, "expert"), None),
            P("expert", None, DP),
            P("expert", None, DP),
            P("expert", DP, None),
            P("expert"),
            P("expert"),
            P(),
        ),
        out_specs=(P(DP, "expert"), P(DP, "expert")),
        check_vma=False,
    )
```

```python
import math

import jax
import jax.numpy as jnp
from jax import lax
from jax.sharding import PartitionSpec as P

HEADS = 32
KVH = 8
HD = 128
EXPERTS = 8
WIN = 32
GROUP_CAP = 24


EPSILON = 1e-05
DP = ("z", "y")


def attend(queries, new_keys, new_values, cache_keys, cache_values):
    span_count, cache_len, kv_width = cache_keys.shape
    kv_local = kv_width // HD
    group = HEADS // KVH
    window = queries.shape[0] // span_count
    query_view = queries.reshape(span_count, window, kv_local, group, HD)
    fresh_keys = new_keys.reshape(span_count, window, kv_local, HD)
    fresh_values = new_values.reshape(span_count, window, kv_local, HD)
    stored_keys = cache_keys.reshape(span_count, cache_len, kv_local, HD)
    stored_values = cache_values.reshape(span_count, cache_len, kv_local, HD)
    factor = 1.0 / math.sqrt(HD)
    past_scores = (
        jnp.einsum("ctkgd,cpkd->ckgtp", query_view, stored_keys, preferred_element_type=jnp.float32)
        * factor
    )
    fresh_scores = (
        jnp.einsum("ctkgd,cskd->ckgts", query_view, fresh_keys, preferred_element_type=jnp.float32)
        * factor
    )
    causal = jnp.arange(window)[:, None] >= jnp.arange(window)[None, :]
    fresh_scores = jnp.where(causal, fresh_scores, -jnp.inf)
    highest = jnp.maximum(jnp.max(past_scores, axis=-1), jnp.max(fresh_scores, axis=-1))[..., None]
    past_exp = jnp.exp(past_scores - highest)
    fresh_exp = jnp.exp(fresh_scores - highest)
    totals = jnp.sum(past_exp, axis=-1, keepdims=True) + jnp.sum(fresh_exp, axis=-1, keepdims=True)
    past_weights = (past_exp / totals).astype(jnp.bfloat16)
    fresh_weights = (fresh_exp / totals).astype(jnp.bfloat16)
    context = jnp.einsum(
        "ckgtp,cpkd->ctkgd", past_weights, stored_values, preferred_element_type=jnp.float32
    )
    context = context + jnp.einsum(
        "ckgts,cskd->ctkgd", fresh_weights, fresh_values, preferred_element_type=jnp.float32
    )
    return context.astype(jnp.bfloat16).reshape(span_count * window, kv_local * group * HD)


def a2a_sum(x, axis, dim, count):
    shape = x.shape
    split = shape[:dim] + (count, shape[dim] // count) + shape[dim + 1:]
    received = lax.all_to_all(x.reshape(split), axis, split_axis=dim, concat_axis=dim, tiled=True)
    return jnp.sum(received, axis=dim)


def a2a_gather(x, axis, count):
    spread = jnp.broadcast_to(x[None], (count,) + x.shape)
    return lax.all_to_all(spread, axis, split_axis=0, concat_axis=0, tiled=True)


def dp_gather(x, axis):
    return lax.all_gather(lax.all_gather(x, "y", axis=axis, tiled=True), "z", axis=axis, tiled=True)


def doubling_sum(x, axis, count):
    step = 1
    while step < count:
        x = x + lax.ppermute(x, axis, [(a, a ^ step) for a in range(count)])
        step *= 2
    return x


def shards(
    residual,
    queries,
    new_keys,
    new_values,
    cache_keys,
    cache_values,
    out_weight,
    ffn_gain,
    router,
    routes,
    w_gate,
    w_up,
    w_down,
    summary_gain,
    reduce_scale,
    assign,
):
    expert_count = lax.axis_size("expert")
    dp_index = lax.axis_index(DP)
    column = lax.axis_index("expert")
    span_local = cache_keys.shape[0]
    tok_local = residual.shape[0]
    width = residual.shape[1]
    slice_width = width // expert_count
    f32_precision = lax.Precision.HIGH
    attended = attend(queries, new_keys, new_values, cache_keys, cache_values)
    y_count = lax.axis_size("y")
    z_count = lax.axis_size("z")
    attended_row = lax.all_gather(attended, "y", axis=0, tiled=True)
    weight_row = a2a_gather(out_weight, "z", z_count)
    col_block = out_weight.shape[1]
    head_terms = jnp.einsum(
        "th,zhc->tzc", attended_row, weight_row, preferred_element_type=jnp.float32
    )
    head_terms = head_terms.reshape(y_count * expert_count, tok_local, z_count * col_block)
    token_cols = lax.all_to_all(
        head_terms, ("y", "expert"), split_axis=0, concat_axis=0, tiled=True
    )
    token_cols = jnp.sum(
        token_cols.reshape(y_count, expert_count, tok_local, z_count * col_block), axis=1
    )
    token_cols = token_cols.reshape(y_count, tok_local, z_count, col_block).transpose(1, 2, 0, 3)
    mixed = residual.astype(jnp.float32) + token_cols.reshape(tok_local, width)
    normed = (
        mixed * lax.rsqrt(jnp.mean(mixed * mixed, axis=-1, keepdims=True) + EPSILON) * ffn_gain
    ).astype(jnp.bfloat16)
    expert_ids = jnp.arange(EXPERTS, dtype=jnp.int32)
    first = routes[:, 0:1] == expert_ids[None, :]
    second = routes[:, 1:2] == expert_ids[None, :]
    partner = jnp.where(first, routes[:, 1:2], jnp.where(second, routes[:, 0:1], -1))
    tag_width = 128
    tag = jnp.broadcast_to(((partner + 1).T)[:, :, None], partner.T.shape + (tag_width,))
    outgoing = jnp.concatenate(
        [jnp.where((partner >= 0).T[:, :, None], normed[None, :, :], 0), tag.astype(jnp.bfloat16)],
        axis=2,
    )
    arrived = lax.all_to_all(outgoing, "expert", split_axis=0, concat_axis=1, tiled=True)
    arrived_rows = arrived[:, :, :width]
    arrived_partner = arrived[:, :, width].astype(jnp.int32) - 1
    present = (arrived_partner >= 0).astype(jnp.int32)
    position = jnp.cumsum(present, axis=1) - 1
    picker = (present[:, None, :] > 0) & (
        position[:, None, :] == jnp.arange(GROUP_CAP)[None, :, None]
    )
    compact = jnp.einsum(
        "eks,esd->ked",
        picker.astype(jnp.bfloat16),
        arrived_rows,
        preferred_element_type=jnp.float32,
    ).astype(jnp.bfloat16)
    arrived_count = arrived_partner.shape[1]
    pick = picker[0]
    slot_present = jnp.any(pick, axis=1)
    slot_partner = jnp.sum(jnp.where(pick, arrived_partner[0][None, :], 0), axis=1)
    local_span = jnp.arange(arrived_count) // WIN
    slot_span = jnp.sum(jnp.where(pick, local_span[None, :], 0), axis=1)
    slot_logits = jnp.dot(compact[:, 0, :], router, preferred_element_type=jnp.float32)
    own_logit = jnp.sum(jnp.where(expert_ids[None, :] == column, slot_logits, 0.0), axis=-1)
    partner_logit = jnp.sum(
        jnp.where(expert_ids[None, :] == slot_partner[:, None], slot_logits, 0.0), axis=-1
    )
    slot_gate = jnp.where(slot_present, jax.nn.sigmoid(own_logit - partner_logit), 0.0)
    pool_weight = jnp.where(
        slot_span[:, None] == jnp.arange(span_local)[None, :], slot_gate[:, None], 0.0
    )
    gathered = dp_gather(compact, 0)
    gathered_weight = lax.all_gather(pool_weight, DP, axis=0, tiled=True)
    n_dp = gathered.shape[0] // GROUP_CAP
    gate_proj = jnp.einsum("ned,edf->nf", gathered, w_gate, preferred_element_type=jnp.float32)
    up_proj = jnp.einsum("ned,edf->nf", gathered, w_up, preferred_element_type=jnp.float32)
    hidden = (jax.nn.silu(gate_proj) * up_proj).astype(jnp.bfloat16)
    span_hidden = jnp.einsum(
        "iks,ikf->isf",
        gathered_weight.reshape(n_dp, GROUP_CAP, span_local),
        hidden.reshape(n_dp, GROUP_CAP, -1).astype(jnp.float32),
        precision=f32_precision,
    ).reshape(n_dp * span_local, -1)
    pooled_part = jnp.dot(
        span_hidden, w_down[0].astype(jnp.float32), precision=f32_precision
    )
    own_span = dp_index * span_local + (column * tok_local) // WIN
    span_count = n_dp * span_local
    mixed_sum = jnp.sum(mixed, axis=0)
    pooled_part = pooled_part + jnp.where(
        (jnp.arange(span_count) == own_span)[:, None], mixed_sum[None, :], 0.0
    )
    pooled_cols = a2a_sum(pooled_part, "expert", 1, expert_count)
    own_cols = a2a_sum(pooled_cols, DP, 0, n_dp)
    squares = doubling_sum(jnp.sum(own_cols * own_cols, axis=-1), "expert", expert_count)
    summary = (
        own_cols * lax.rsqrt(squares / width + EPSILON)[:, None] * summary_gain
    ).astype(jnp.bfloat16)
    everyone = a2a_gather(summary, DP, n_dp).reshape(n_dp * span_local, slice_width)
    heads_local = slice_width // HD
    mine = summary.reshape(span_local, heads_local, HD)
    others = everyone.reshape(everyone.shape[0], heads_local, HD)
    factor = reduce_scale / math.sqrt(HD)
    scores = (
        jnp.einsum("chd,khd->hck", mine, others, preferred_element_type=jnp.float32)
        * factor[:, None, None]
    )
    own_assign = lax.dynamic_slice_in_dim(assign, dp_index * span_local, span_local)
    same = own_assign[:, None] == assign[None, :]
    scores = jnp.where(same[None], scores, -jnp.inf)
    highest = jnp.max(scores, axis=-1, keepdims=True)
    expo = jnp.exp(scores - highest)
    weights = (expo / jnp.sum(expo, axis=-1, keepdims=True)).astype(jnp.bfloat16)
    reduced = jnp.einsum("hck,khd->chd", weights, others, preferred_element_type=jnp.float32)
    reduced = reduced.reshape(span_local, slice_width).astype(jnp.bfloat16)
    return (summary, reduced)


def solution(mesh):
    dp_size, expert_size = mesh.devices.shape
    y_size = 4
    split_mesh = jax.sharding.Mesh(
        mesh.devices.reshape(dp_size // y_size, y_size, expert_size), ("z", "y", "expert")
    )
    return jax.shard_map(
        shards,
        mesh=split_mesh,
        in_specs=(
            P((*DP, "expert"), None),
            P(DP, "expert"),
            P(DP, "expert"),
            P(DP, "expert"),
            P(DP, None, "expert"),
            P(DP, None, "expert"),
            P("expert", DP),
            P(),
            P(),
            P((*DP, "expert"), None),
            P("expert", None, DP),
            P("expert", None, DP),
            P("expert", DP, None),
            P("expert"),
            P("expert"),
            P(),
        ),
        out_specs=(P(DP, "expert"), P(DP, "expert")),
        check_vma=False,
    )
```

```python
import math

import jax
import jax.numpy as jnp
from jax import lax
from jax.sharding import PartitionSpec as P

HEADS = 32
KVH = 8
HD = 128
EXPERTS = 8
WIN = 32
GROUP_CAP = 24


EPSILON = 1e-05
DP = ("z", "y")


def attend(queries, new_keys, new_values, cache_keys, cache_values):
    span_count, cache_len, kv_width = cache_keys.shape
    kv_local = kv_width // HD
    group = HEADS // KVH
    window = queries.shape[0] // span_count
    query_view = queries.reshape(span_count, window, kv_local, group, HD)
    fresh_keys = new_keys.reshape(span_count, window, kv_local, HD)
    fresh_values = new_values.reshape(span_count, window, kv_local, HD)
    stored_keys = cache_keys.reshape(span_count, cache_len, kv_local, HD)
    stored_values = cache_values.reshape(span_count, cache_len, kv_local, HD)
    factor = 1.0 / math.sqrt(HD)
    past_scores = (
        jnp.einsum("ctkgd,cpkd->ckgtp", query_view, stored_keys, preferred_element_type=jnp.float32)
        * factor
    )
    fresh_scores = (
        jnp.einsum("ctkgd,cskd->ckgts", query_view, fresh_keys, preferred_element_type=jnp.float32)
        * factor
    )
    causal = jnp.arange(window)[:, None] >= jnp.arange(window)[None, :]
    fresh_scores = jnp.where(causal, fresh_scores, -jnp.inf)
    highest = jnp.maximum(jnp.max(past_scores, axis=-1), jnp.max(fresh_scores, axis=-1))[..., None]
    past_exp = jnp.exp(past_scores - highest)
    fresh_exp = jnp.exp(fresh_scores - highest)
    totals = jnp.sum(past_exp, axis=-1, keepdims=True) + jnp.sum(fresh_exp, axis=-1, keepdims=True)
    past_weights = (past_exp / totals).astype(jnp.bfloat16)
    fresh_weights = (fresh_exp / totals).astype(jnp.bfloat16)
    context = jnp.einsum(
        "ckgtp,cpkd->ctkgd", past_weights, stored_values, preferred_element_type=jnp.float32
    )
    context = context + jnp.einsum(
        "ckgts,cskd->ctkgd", fresh_weights, fresh_values, preferred_element_type=jnp.float32
    )
    return context.astype(jnp.bfloat16).reshape(span_count * window, kv_local * group * HD)


def a2a_sum(x, axis, dim, count):
    shape = x.shape
    split = shape[:dim] + (count, shape[dim] // count) + shape[dim + 1:]
    received = lax.all_to_all(x.reshape(split), axis, split_axis=dim, concat_axis=dim, tiled=True)
    return jnp.sum(received, axis=dim)


def a2a_gather(x, axis, count):
    spread = jnp.broadcast_to(x[None], (count,) + x.shape)
    return lax.all_to_all(spread, axis, split_axis=0, concat_axis=0, tiled=True)


def dp_gather(x, axis):
    assert axis == 0
    row = a2a_gather(x, "y", lax.axis_size("y"))
    row = row.reshape((row.shape[0] * row.shape[1],) + row.shape[2:])
    return lax.all_gather(row, "z", axis=0, tiled=True)


def doubling_sum(x, axis, count):
    step = 1
    while step < count:
        x = x + lax.ppermute(x, axis, [(a, a ^ step) for a in range(count)])
        step *= 2
    return x


def shards(
    residual,
    queries,
    new_keys,
    new_values,
    cache_keys,
    cache_values,
    out_weight,
    ffn_gain,
    router,
    routes,
    w_gate,
    w_up,
    w_down,
    summary_gain,
    reduce_scale,
    assign,
):
    expert_count = lax.axis_size("expert")
    dp_index = lax.axis_index(DP)
    column = lax.axis_index("expert")
    span_local = cache_keys.shape[0]
    tok_local = residual.shape[0]
    width = residual.shape[1]
    slice_width = width // expert_count
    f32_precision = lax.Precision.HIGH
    attended = attend(queries, new_keys, new_values, cache_keys, cache_values)
    y_count = lax.axis_size("y")
    z_count = lax.axis_size("z")
    attended_row = lax.all_gather(attended, "y", axis=0, tiled=True)
    weight_row = a2a_gather(out_weight, "z", z_count)
    col_block = out_weight.shape[1]
    head_terms = jnp.einsum(
        "th,zhc->tzc", attended_row, weight_row, preferred_element_type=jnp.float32
    )
    head_terms = head_terms.reshape(y_count * expert_count, tok_local, z_count * col_block)
    token_cols = lax.all_to_all(
        head_terms, ("y", "expert"), split_axis=0, concat_axis=0, tiled=True
    )
    token_cols = jnp.sum(
        token_cols.reshape(y_count, expert_count, tok_local, z_count * col_block), axis=1
    )
    token_cols = token_cols.reshape(y_count, tok_local, z_count, col_block).transpose(1, 2, 0, 3)
    mixed = residual.astype(jnp.float32) + token_cols.reshape(tok_local, width)
    normed = (
        mixed * lax.rsqrt(jnp.mean(mixed * mixed, axis=-1, keepdims=True) + EPSILON) * ffn_gain
    ).astype(jnp.bfloat16)
    expert_ids = jnp.arange(EXPERTS, dtype=jnp.int32)
    first = routes[:, 0:1] == expert_ids[None, :]
    second = routes[:, 1:2] == expert_ids[None, :]
    partner = jnp.where(first, routes[:, 1:2], jnp.where(second, routes[:, 0:1], -1))
    tag_width = 128
    tag = jnp.broadcast_to(((partner + 1).T)[:, :, None], partner.T.shape + (tag_width,))
    outgoing = jnp.concatenate(
        [jnp.where((partner >= 0).T[:, :, None], normed[None, :, :], 0), tag.astype(jnp.bfloat16)],
        axis=2,
    )
    arrived = lax.all_to_all(outgoing, "expert", split_axis=0, concat_axis=1, tiled=True)
    arrived_rows = arrived[:, :, :width]
    arrived_partner = arrived[:, :, width].astype(jnp.int32) - 1
    present = (arrived_partner >= 0).astype(jnp.int32)
    position = jnp.cumsum(present, axis=1) - 1
    picker = (present[:, None, :] > 0) & (
        position[:, None, :] == jnp.arange(GROUP_CAP)[None, :, None]
    )
    compact = jnp.einsum(
        "eks,esd->ked",
        picker.astype(jnp.bfloat16),
        arrived_rows,
        preferred_element_type=jnp.float32,
    ).astype(jnp.bfloat16)
    arrived_count = arrived_partner.shape[1]
    pick = picker[0]
    slot_present = jnp.any(pick, axis=1)
    slot_partner = jnp.sum(jnp.where(pick, arrived_partner[0][None, :], 0), axis=1)
    local_span = jnp.arange(arrived_count) // WIN
    slot_span = jnp.sum(jnp.where(pick, local_span[None, :], 0), axis=1)
    slot_logits = jnp.dot(compact[:, 0, :], router, preferred_element_type=jnp.float32)
    own_logit = jnp.sum(jnp.where(expert_ids[None, :] == column, slot_logits, 0.0), axis=-1)
    partner_logit = jnp.sum(
        jnp.where(expert_ids[None, :] == slot_partner[:, None], slot_logits, 0.0), axis=-1
    )
    slot_gate = jnp.where(slot_present, jax.nn.sigmoid(own_logit - partner_logit), 0.0)
    pool_weight = jnp.where(
        slot_span[:, None] == jnp.arange(span_local)[None, :], slot_gate[:, None], 0.0
    )
    gathered = dp_gather(compact, 0)
    gathered_weight = lax.all_gather(pool_weight, DP, axis=0, tiled=True)
    n_dp = gathered.shape[0] // GROUP_CAP
    gate_proj = jnp.einsum("ned,edf->nf", gathered, w_gate, preferred_element_type=jnp.float32)
    up_proj = jnp.einsum("ned,edf->nf", gathered, w_up, preferred_element_type=jnp.float32)
    hidden = (jax.nn.silu(gate_proj) * up_proj).astype(jnp.bfloat16)
    span_hidden = jnp.einsum(
        "iks,ikf->isf",
        gathered_weight.reshape(n_dp, GROUP_CAP, span_local),
        hidden.reshape(n_dp, GROUP_CAP, -1).astype(jnp.float32),
        precision=f32_precision,
    ).reshape(n_dp * span_local, -1)
    pooled_part = jnp.dot(
        span_hidden, w_down[0].astype(jnp.float32), precision=f32_precision
    )
    own_span = dp_index * span_local + (column * tok_local) // WIN
    span_count = n_dp * span_local
    mixed_sum = jnp.sum(mixed, axis=0)
    pooled_part = pooled_part + jnp.where(
        (jnp.arange(span_count) == own_span)[:, None], mixed_sum[None, :], 0.0
    )
    pooled_part = pooled_part.reshape(n_dp, span_local, expert_count, slice_width)
    pooled_part = pooled_part.transpose(0, 2, 1, 3).reshape(
        n_dp * expert_count, span_local, slice_width
    )
    own_cols = jnp.sum(
        lax.all_to_all(pooled_part, (*DP, "expert"), split_axis=0, concat_axis=0, tiled=True),
        axis=0,
    )
    squares = doubling_sum(jnp.sum(own_cols * own_cols, axis=-1), "expert", expert_count)
    summary = (
        own_cols * lax.rsqrt(squares / width + EPSILON)[:, None] * summary_gain
    ).astype(jnp.bfloat16)
    everyone = a2a_gather(summary, DP, n_dp).reshape(n_dp * span_local, slice_width)
    heads_local = slice_width // HD
    mine = summary.reshape(span_local, heads_local, HD)
    others = everyone.reshape(everyone.shape[0], heads_local, HD)
    factor = reduce_scale / math.sqrt(HD)
    scores = (
        jnp.einsum("chd,khd->hck", mine, others, preferred_element_type=jnp.float32)
        * factor[:, None, None]
    )
    own_assign = lax.dynamic_slice_in_dim(assign, dp_index * span_local, span_local)
    same = own_assign[:, None] == assign[None, :]
    scores = jnp.where(same[None], scores, -jnp.inf)
    highest = jnp.max(scores, axis=-1, keepdims=True)
    expo = jnp.exp(scores - highest)
    weights = (expo / jnp.sum(expo, axis=-1, keepdims=True)).astype(jnp.bfloat16)
    reduced = jnp.einsum("hck,khd->chd", weights, others, preferred_element_type=jnp.float32)
    reduced = reduced.reshape(span_local, slice_width).astype(jnp.bfloat16)
    return (summary, reduced)


def solution(mesh):
    dp_size, expert_size = mesh.devices.shape
    y_size = 4
    split_mesh = jax.sharding.Mesh(
        mesh.devices.reshape(dp_size // y_size, y_size, expert_size), ("z", "y", "expert")
    )
    return jax.shard_map(
        shards,
        mesh=split_mesh,
        in_specs=(
            P((*DP, "expert"), None),
            P(DP, "expert"),
            P(DP, "expert"),
            P(DP, "expert"),
            P(DP, None, "expert"),
            P(DP, None, "expert"),
            P("expert", DP),
            P(),
            P(),
            P((*DP, "expert"), None),
            P("expert", None, DP),
            P("expert", None, DP),
            P("expert", DP, None),
            P("expert"),
            P("expert"),
            P(),
        ),
        out_specs=(P(DP, "expert"), P(DP, "expert")),
        check_vma=False,
    )
```

```python
import math

import jax
import jax.numpy as jnp
from jax import lax
from jax.sharding import PartitionSpec as P

HEADS = 32
KVH = 8
HD = 128
EXPERTS = 8
WIN = 32
GROUP_CAP = 24


EPSILON = 1e-05
DP = ("z", "y")


def attend(queries, new_keys, new_values, cache_keys, cache_values):
    span_count, cache_len, kv_width = cache_keys.shape
    kv_local = kv_width // HD
    group = HEADS // KVH
    window = queries.shape[0] // span_count
    query_view = queries.reshape(span_count, window, kv_local, group, HD)
    fresh_keys = new_keys.reshape(span_count, window, kv_local, HD)
    fresh_values = new_values.reshape(span_count, window, kv_local, HD)
    stored_keys = cache_keys.reshape(span_count, cache_len, kv_local, HD)
    stored_values = cache_values.reshape(span_count, cache_len, kv_local, HD)
    factor = 1.0 / math.sqrt(HD)
    past_scores = (
        jnp.einsum("ctkgd,cpkd->ckgtp", query_view, stored_keys, preferred_element_type=jnp.float32)
        * factor
    )
    fresh_scores = (
        jnp.einsum("ctkgd,cskd->ckgts", query_view, fresh_keys, preferred_element_type=jnp.float32)
        * factor
    )
    causal = jnp.arange(window)[:, None] >= jnp.arange(window)[None, :]
    fresh_scores = jnp.where(causal, fresh_scores, -jnp.inf)
    highest = jnp.maximum(jnp.max(past_scores, axis=-1), jnp.max(fresh_scores, axis=-1))[..., None]
    past_exp = jnp.exp(past_scores - highest)
    fresh_exp = jnp.exp(fresh_scores - highest)
    totals = jnp.sum(past_exp, axis=-1, keepdims=True) + jnp.sum(fresh_exp, axis=-1, keepdims=True)
    past_weights = (past_exp / totals).astype(jnp.bfloat16)
    fresh_weights = (fresh_exp / totals).astype(jnp.bfloat16)
    context = jnp.einsum(
        "ckgtp,cpkd->ctkgd", past_weights, stored_values, preferred_element_type=jnp.float32
    )
    context = context + jnp.einsum(
        "ckgts,cskd->ctkgd", fresh_weights, fresh_values, preferred_element_type=jnp.float32
    )
    return context.astype(jnp.bfloat16).reshape(span_count * window, kv_local * group * HD)


def a2a_sum(x, axis, dim, count):
    shape = x.shape
    split = shape[:dim] + (count, shape[dim] // count) + shape[dim + 1:]
    received = lax.all_to_all(x.reshape(split), axis, split_axis=dim, concat_axis=dim, tiled=True)
    return jnp.sum(received, axis=dim)


def a2a_gather(x, axis, count):
    spread = jnp.broadcast_to(x[None], (count,) + x.shape)
    return lax.all_to_all(spread, axis, split_axis=0, concat_axis=0, tiled=True)


def dp_gather(x, axis):
    return lax.all_gather(lax.all_gather(x, "y", axis=axis, tiled=True), "z", axis=axis, tiled=True)


def doubling_sum(x, axis, count):
    step = 1
    while step < count:
        x = x + lax.ppermute(x, axis, [(a, a ^ step) for a in range(count)])
        step *= 2
    return x


def shards(
    residual,
    queries,
    new_keys,
    new_values,
    cache_keys,
    cache_values,
    out_weight,
    ffn_gain,
    router,
    routes,
    w_gate,
    w_up,
    w_down,
    summary_gain,
    reduce_scale,
    assign,
):
    expert_count = lax.axis_size("expert")
    dp_index = lax.axis_index(DP)
    column = lax.axis_index("expert")
    span_local = cache_keys.shape[0]
    tok_local = residual.shape[0]
    width = residual.shape[1]
    slice_width = width // expert_count
    f32_precision = lax.Precision.HIGH
    attended = attend(queries, new_keys, new_values, cache_keys, cache_values)
    y_count = lax.axis_size("y")
    z_count = lax.axis_size("z")
    attended_row = lax.all_gather(attended, "y", axis=0, tiled=True)
    weight_row = a2a_gather(out_weight, "z", z_count)
    col_block = out_weight.shape[1]
    head_terms = jnp.einsum(
        "th,zhc->tzc", attended_row, weight_row, preferred_element_type=jnp.float32
    )
    head_terms = head_terms.reshape(y_count * expert_count, tok_local, z_count * col_block)
    token_cols = lax.all_to_all(
        head_terms, ("y", "expert"), split_axis=0, concat_axis=0, tiled=True
    )
    token_cols = jnp.sum(
        token_cols.reshape(y_count, expert_count, tok_local, z_count * col_block), axis=1
    )
    token_cols = token_cols.reshape(y_count, tok_local, z_count, col_block).transpose(1, 2, 0, 3)
    mixed = residual.astype(jnp.float32) + token_cols.reshape(tok_local, width)
    normed = (
        mixed * lax.rsqrt(jnp.mean(mixed * mixed, axis=-1, keepdims=True) + EPSILON) * ffn_gain
    ).astype(jnp.bfloat16)
    expert_ids = jnp.arange(EXPERTS, dtype=jnp.int32)
    first = routes[:, 0:1] == expert_ids[None, :]
    second = routes[:, 1:2] == expert_ids[None, :]
    partner = jnp.where(first, routes[:, 1:2], jnp.where(second, routes[:, 0:1], -1))
    tag_width = 128
    tag = jnp.broadcast_to(((partner + 1).T)[:, :, None], partner.T.shape + (tag_width,))
    outgoing = jnp.concatenate(
        [jnp.where((partner >= 0).T[:, :, None], normed[None, :, :], 0), tag.astype(jnp.bfloat16)],
        axis=2,
    )
    arrived = lax.all_to_all(outgoing, "expert", split_axis=0, concat_axis=1, tiled=True)
    arrived_rows = arrived[:, :, :width]
    arrived_partner = arrived[:, :, width].astype(jnp.int32) - 1
    present = (arrived_partner >= 0).astype(jnp.int32)
    position = jnp.cumsum(present, axis=1) - 1
    picker = (present[:, None, :] > 0) & (
        position[:, None, :] == jnp.arange(GROUP_CAP)[None, :, None]
    )
    compact = jnp.einsum(
        "eks,esd->ked",
        picker.astype(jnp.bfloat16),
        arrived_rows,
        preferred_element_type=jnp.float32,
    ).astype(jnp.bfloat16)
    arrived_count = arrived_partner.shape[1]
    pick = picker[0]
    slot_present = jnp.any(pick, axis=1)
    slot_partner = jnp.sum(jnp.where(pick, arrived_partner[0][None, :], 0), axis=1)
    local_span = jnp.arange(arrived_count) // WIN
    slot_span = jnp.sum(jnp.where(pick, local_span[None, :], 0), axis=1)
    slot_logits = jnp.dot(compact[:, 0, :], router, preferred_element_type=jnp.float32)
    own_logit = jnp.sum(jnp.where(expert_ids[None, :] == column, slot_logits, 0.0), axis=-1)
    partner_logit = jnp.sum(
        jnp.where(expert_ids[None, :] == slot_partner[:, None], slot_logits, 0.0), axis=-1
    )
    slot_gate = jnp.where(slot_present, jax.nn.sigmoid(own_logit - partner_logit), 0.0)
    pool_weight = jnp.where(
        slot_span[:, None] == jnp.arange(span_local)[None, :], slot_gate[:, None], 0.0
    )
    gathered = dp_gather(compact, 0)
    gathered_weight = lax.all_gather(pool_weight, DP, axis=0, tiled=True)
    n_dp = gathered.shape[0] // GROUP_CAP
    gate_proj = jnp.einsum("ned,edf->nf", gathered, w_gate, preferred_element_type=jnp.float32)
    up_proj = jnp.einsum("ned,edf->nf", gathered, w_up, preferred_element_type=jnp.float32)
    hidden = (jax.nn.silu(gate_proj) * up_proj).astype(jnp.bfloat16)
    span_hidden = jnp.einsum(
        "iks,ikf->isf",
        gathered_weight.reshape(n_dp, GROUP_CAP, span_local),
        hidden.reshape(n_dp, GROUP_CAP, -1).astype(jnp.float32),
        precision=f32_precision,
    ).reshape(n_dp * span_local, -1)
    pooled_part = jnp.dot(
        span_hidden, w_down[0].astype(jnp.float32), precision=f32_precision
    )
    own_span = dp_index * span_local + (column * tok_local) // WIN
    span_count = n_dp * span_local
    mixed_sum = jnp.sum(mixed, axis=0)
    pooled_part = pooled_part + jnp.where(
        (jnp.arange(span_count) == own_span)[:, None], mixed_sum[None, :], 0.0
    )
    pooled_part = pooled_part.reshape(z_count, y_count, span_local, expert_count, slice_width)
    pooled_part = pooled_part.transpose(1, 3, 0, 2, 4).reshape(
        y_count * expert_count, z_count * span_local, slice_width
    )
    plane_cols = jnp.sum(
        lax.all_to_all(pooled_part, ("y", "expert"), split_axis=0, concat_axis=0, tiled=True),
        axis=0,
    )
    own_cols = jnp.sum(
        lax.all_to_all(
            plane_cols.reshape(z_count, span_local, slice_width),
            "z",
            split_axis=0,
            concat_axis=0,
            tiled=True,
        ),
        axis=0,
    )
    squares = doubling_sum(jnp.sum(own_cols * own_cols, axis=-1), "expert", expert_count)
    summary = (
        own_cols * lax.rsqrt(squares / width + EPSILON)[:, None] * summary_gain
    ).astype(jnp.bfloat16)
    everyone = a2a_gather(summary, DP, n_dp).reshape(n_dp * span_local, slice_width)
    heads_local = slice_width // HD
    mine = summary.reshape(span_local, heads_local, HD)
    others = everyone.reshape(everyone.shape[0], heads_local, HD)
    factor = reduce_scale / math.sqrt(HD)
    scores = (
        jnp.einsum("chd,khd->hck", mine, others, preferred_element_type=jnp.float32)
        * factor[:, None, None]
    )
    own_assign = lax.dynamic_slice_in_dim(assign, dp_index * span_local, span_local)
    same = own_assign[:, None] == assign[None, :]
    scores = jnp.where(same[None], scores, -jnp.inf)
    highest = jnp.max(scores, axis=-1, keepdims=True)
    expo = jnp.exp(scores - highest)
    weights = (expo / jnp.sum(expo, axis=-1, keepdims=True)).astype(jnp.bfloat16)
    reduced = jnp.einsum("hck,khd->chd", weights, others, preferred_element_type=jnp.float32)
    reduced = reduced.reshape(span_local, slice_width).astype(jnp.bfloat16)
    return (summary, reduced)


def solution(mesh):
    dp_size, expert_size = mesh.devices.shape
    y_size = 4
    split_mesh = jax.sharding.Mesh(
        mesh.devices.reshape(dp_size // y_size, y_size, expert_size), ("z", "y", "expert")
    )
    return jax.shard_map(
        shards,
        mesh=split_mesh,
        in_specs=(
            P((*DP, "expert"), None),
            P(DP, "expert"),
            P(DP, "expert"),
            P(DP, "expert"),
            P(DP, None, "expert"),
            P(DP, None, "expert"),
            P("expert", DP),
            P(),
            P(),
            P((*DP, "expert"), None),
            P("expert", None, DP),
            P("expert", None, DP),
            P("expert", DP, None),
            P("expert"),
            P("expert"),
            P(),
        ),
        out_specs=(P(DP, "expert"), P(DP, "expert")),
        check_vma=False,
    )
```

```python
import math

import jax
import jax.numpy as jnp
from jax import lax
from jax.sharding import PartitionSpec as P

HEADS = 32
KVH = 8
HD = 128
EXPERTS = 8
WIN = 32
GROUP_CAP = 24


EPSILON = 1e-05
DP = ("z", "y")


def attend(queries, new_keys, new_values, cache_keys, cache_values):
    span_count, cache_len, kv_width = cache_keys.shape
    kv_local = kv_width // HD
    group = HEADS // KVH
    window = queries.shape[0] // span_count
    query_view = queries.reshape(span_count, window, kv_local, group, HD)
    fresh_keys = new_keys.reshape(span_count, window, kv_local, HD)
    fresh_values = new_values.reshape(span_count, window, kv_local, HD)
    stored_keys = cache_keys.reshape(span_count, cache_len, kv_local, HD)
    stored_values = cache_values.reshape(span_count, cache_len, kv_local, HD)
    factor = 1.0 / math.sqrt(HD)
    past_scores = (
        jnp.einsum("ctkgd,cpkd->ckgtp", query_view, stored_keys, preferred_element_type=jnp.float32)
        * factor
    )
    fresh_scores = (
        jnp.einsum("ctkgd,cskd->ckgts", query_view, fresh_keys, preferred_element_type=jnp.float32)
        * factor
    )
    causal = jnp.arange(window)[:, None] >= jnp.arange(window)[None, :]
    fresh_scores = jnp.where(causal, fresh_scores, -jnp.inf)
    highest = jnp.maximum(jnp.max(past_scores, axis=-1), jnp.max(fresh_scores, axis=-1))[..., None]
    past_exp = jnp.exp(past_scores - highest)
    fresh_exp = jnp.exp(fresh_scores - highest)
    totals = jnp.sum(past_exp, axis=-1, keepdims=True) + jnp.sum(fresh_exp, axis=-1, keepdims=True)
    past_weights = (past_exp / totals).astype(jnp.bfloat16)
    fresh_weights = (fresh_exp / totals).astype(jnp.bfloat16)
    context = jnp.einsum(
        "ckgtp,cpkd->ctkgd", past_weights, stored_values, preferred_element_type=jnp.float32
    )
    context = context + jnp.einsum(
        "ckgts,cskd->ctkgd", fresh_weights, fresh_values, preferred_element_type=jnp.float32
    )
    return context.astype(jnp.bfloat16).reshape(span_count * window, kv_local * group * HD)


def a2a_sum(x, axis, dim, count):
    shape = x.shape
    split = shape[:dim] + (count, shape[dim] // count) + shape[dim + 1:]
    received = lax.all_to_all(x.reshape(split), axis, split_axis=dim, concat_axis=dim, tiled=True)
    return jnp.sum(received, axis=dim)


def a2a_gather(x, axis, count):
    spread = jnp.broadcast_to(x[None], (count,) + x.shape)
    return lax.all_to_all(spread, axis, split_axis=0, concat_axis=0, tiled=True)


def dp_gather(x, axis):
    return lax.all_gather(lax.all_gather(x, "y", axis=axis, tiled=True), "z", axis=axis, tiled=True)


def ring_gather(x, axis, count):
    me = lax.axis_index(axis)
    to_next = [(a, (a + 1) % count) for a in range(count)]
    to_prev = [(a, (a - 1) % count) for a in range(count)]
    from_prev, from_next = x, x
    by_offset = {0: x}
    for step in range(1, count // 2 + 1):
        from_prev = lax.ppermute(from_prev, axis, to_next)
        by_offset[(count - step) % count] = from_prev
        if step < count - step:
            from_next = lax.ppermute(from_next, axis, to_prev)
            by_offset[step] = from_next
    relative = jnp.stack([by_offset[d] for d in range(count)])
    return jnp.roll(relative, me, axis=0)


def doubling_sum(x, axis, count):
    step = 1
    while step < count:
        x = x + lax.ppermute(x, axis, [(a, a ^ step) for a in range(count)])
        step *= 2
    return x


def shards(
    residual,
    queries,
    new_keys,
    new_values,
    cache_keys,
    cache_values,
    out_weight,
    ffn_gain,
    router,
    routes,
    w_gate,
    w_up,
    w_down,
    summary_gain,
    reduce_scale,
    assign,
):
    expert_count = lax.axis_size("expert")
    dp_index = lax.axis_index(DP)
    column = lax.axis_index("expert")
    span_local = cache_keys.shape[0]
    tok_local = residual.shape[0]
    width = residual.shape[1]
    slice_width = width // expert_count
    f32_precision = lax.Precision.HIGH
    attended = attend(queries, new_keys, new_values, cache_keys, cache_values)
    y_count = lax.axis_size("y")
    z_count = lax.axis_size("z")
    attended_row = lax.all_gather(attended, "y", axis=0, tiled=True)
    weight_row = ring_gather(out_weight, "z", z_count)
    col_block = out_weight.shape[1]
    head_terms = jnp.einsum(
        "th,zhc->tzc", attended_row, weight_row, preferred_element_type=jnp.float32
    )
    head_terms = head_terms.reshape(y_count * expert_count, tok_local, z_count * col_block)
    token_cols = lax.all_to_all(
        head_terms, ("y", "expert"), split_axis=0, concat_axis=0, tiled=True
    )
    token_cols = jnp.sum(
        token_cols.reshape(y_count, expert_count, tok_local, z_count * col_block), axis=1
    )
    token_cols = token_cols.reshape(y_count, tok_local, z_count, col_block).transpose(1, 2, 0, 3)
    mixed = residual.astype(jnp.float32) + token_cols.reshape(tok_local, width)
    normed = (
        mixed * lax.rsqrt(jnp.mean(mixed * mixed, axis=-1, keepdims=True) + EPSILON) * ffn_gain
    ).astype(jnp.bfloat16)
    expert_ids = jnp.arange(EXPERTS, dtype=jnp.int32)
    first = routes[:, 0:1] == expert_ids[None, :]
    second = routes[:, 1:2] == expert_ids[None, :]
    partner = jnp.where(first, routes[:, 1:2], jnp.where(second, routes[:, 0:1], -1))
    tag_width = 128
    tag = jnp.broadcast_to(((partner + 1).T)[:, :, None], partner.T.shape + (tag_width,))
    outgoing = jnp.concatenate(
        [jnp.where((partner >= 0).T[:, :, None], normed[None, :, :], 0), tag.astype(jnp.bfloat16)],
        axis=2,
    )
    arrived = lax.all_to_all(outgoing, "expert", split_axis=0, concat_axis=1, tiled=True)
    arrived_rows = arrived[:, :, :width]
    arrived_partner = arrived[:, :, width].astype(jnp.int32) - 1
    present = (arrived_partner >= 0).astype(jnp.int32)
    position = jnp.cumsum(present, axis=1) - 1
    picker = (present[:, None, :] > 0) & (
        position[:, None, :] == jnp.arange(GROUP_CAP)[None, :, None]
    )
    compact = jnp.einsum(
        "eks,esd->ked",
        picker.astype(jnp.bfloat16),
        arrived_rows,
        preferred_element_type=jnp.float32,
    ).astype(jnp.bfloat16)
    arrived_count = arrived_partner.shape[1]
    pick = picker[0]
    slot_present = jnp.any(pick, axis=1)
    slot_partner = jnp.sum(jnp.where(pick, arrived_partner[0][None, :], 0), axis=1)
    local_span = jnp.arange(arrived_count) // WIN
    slot_span = jnp.sum(jnp.where(pick, local_span[None, :], 0), axis=1)
    slot_logits = jnp.dot(compact[:, 0, :], router, preferred_element_type=jnp.float32)
    own_logit = jnp.sum(jnp.where(expert_ids[None, :] == column, slot_logits, 0.0), axis=-1)
    partner_logit = jnp.sum(
        jnp.where(expert_ids[None, :] == slot_partner[:, None], slot_logits, 0.0), axis=-1
    )
    slot_gate = jnp.where(slot_present, jax.nn.sigmoid(own_logit - partner_logit), 0.0)
    pool_weight = jnp.where(
        slot_span[:, None] == jnp.arange(span_local)[None, :], slot_gate[:, None], 0.0
    )
    gathered = dp_gather(compact, 0)
    gathered_weight = lax.all_gather(pool_weight, DP, axis=0, tiled=True)
    n_dp = gathered.shape[0] // GROUP_CAP
    gate_proj = jnp.einsum("ned,edf->nf", gathered, w_gate, preferred_element_type=jnp.float32)
    up_proj = jnp.einsum("ned,edf->nf", gathered, w_up, preferred_element_type=jnp.float32)
    hidden = (jax.nn.silu(gate_proj) * up_proj).astype(jnp.bfloat16)
    span_hidden = jnp.einsum(
        "iks,ikf->isf",
        gathered_weight.reshape(n_dp, GROUP_CAP, span_local),
        hidden.reshape(n_dp, GROUP_CAP, -1).astype(jnp.float32),
        precision=f32_precision,
    ).reshape(n_dp * span_local, -1)
    pooled_part = jnp.dot(
        span_hidden, w_down[0].astype(jnp.float32), precision=f32_precision
    )
    own_span = dp_index * span_local + (column * tok_local) // WIN
    span_count = n_dp * span_local
    mixed_sum = jnp.sum(mixed, axis=0)
    pooled_part = pooled_part + jnp.where(
        (jnp.arange(span_count) == own_span)[:, None], mixed_sum[None, :], 0.0
    )
    pooled_cols = a2a_sum(pooled_part, "expert", 1, expert_count)
    own_cols = a2a_sum(pooled_cols, DP, 0, n_dp)
    squares = doubling_sum(jnp.sum(own_cols * own_cols, axis=-1), "expert", expert_count)
    summary = (
        own_cols * lax.rsqrt(squares / width + EPSILON)[:, None] * summary_gain
    ).astype(jnp.bfloat16)
    everyone = a2a_gather(summary, DP, n_dp).reshape(n_dp * span_local, slice_width)
    heads_local = slice_width // HD
    mine = summary.reshape(span_local, heads_local, HD)
    others = everyone.reshape(everyone.shape[0], heads_local, HD)
    factor = reduce_scale / math.sqrt(HD)
    scores = (
        jnp.einsum("chd,khd->hck", mine, others, preferred_element_type=jnp.float32)
        * factor[:, None, None]
    )
    own_assign = lax.dynamic_slice_in_dim(assign, dp_index * span_local, span_local)
    same = own_assign[:, None] == assign[None, :]
    scores = jnp.where(same[None], scores, -jnp.inf)
    highest = jnp.max(scores, axis=-1, keepdims=True)
    expo = jnp.exp(scores - highest)
    weights = (expo / jnp.sum(expo, axis=-1, keepdims=True)).astype(jnp.bfloat16)
    reduced = jnp.einsum("hck,khd->chd", weights, others, preferred_element_type=jnp.float32)
    reduced = reduced.reshape(span_local, slice_width).astype(jnp.bfloat16)
    return (summary, reduced)


def solution(mesh):
    dp_size, expert_size = mesh.devices.shape
    y_size = 4
    split_mesh = jax.sharding.Mesh(
        mesh.devices.reshape(dp_size // y_size, y_size, expert_size), ("z", "y", "expert")
    )
    return jax.shard_map(
        shards,
        mesh=split_mesh,
        in_specs=(
            P((*DP, "expert"), None),
            P(DP, "expert"),
            P(DP, "expert"),
            P(DP, "expert"),
            P(DP, None, "expert"),
            P(DP, None, "expert"),
            P("expert", DP),
            P(),
            P(),
            P((*DP, "expert"), None),
            P("expert", None, DP),
            P("expert", None, DP),
            P("expert", DP, None),
            P("expert"),
            P("expert"),
            P(),
        ),
        out_specs=(P(DP, "expert"), P(DP, "expert")),
        check_vma=False,
    )
```

```python
import math

import jax
import jax.numpy as jnp
from jax import lax
from jax.sharding import PartitionSpec as P

HEADS = 32
KVH = 8
HD = 128
EXPERTS = 8
WIN = 32
GROUP_CAP = 24


EPSILON = 1e-05
DP = ("z", "y")


def attend(queries, new_keys, new_values, cache_keys, cache_values):
    span_count, cache_len, kv_width = cache_keys.shape
    kv_local = kv_width // HD
    group = HEADS // KVH
    window = queries.shape[0] // span_count
    query_view = queries.reshape(span_count, window, kv_local, group, HD)
    fresh_keys = new_keys.reshape(span_count, window, kv_local, HD)
    fresh_values = new_values.reshape(span_count, window, kv_local, HD)
    stored_keys = cache_keys.reshape(span_count, cache_len, kv_local, HD)
    stored_values = cache_values.reshape(span_count, cache_len, kv_local, HD)
    factor = 1.0 / math.sqrt(HD)
    past_scores = (
        jnp.einsum("ctkgd,cpkd->ckgtp", query_view, stored_keys, preferred_element_type=jnp.float32)
        * factor
    )
    fresh_scores = (
        jnp.einsum("ctkgd,cskd->ckgts", query_view, fresh_keys, preferred_element_type=jnp.float32)
        * factor
    )
    causal = jnp.arange(window)[:, None] >= jnp.arange(window)[None, :]
    fresh_scores = jnp.where(causal, fresh_scores, -jnp.inf)
    highest = jnp.maximum(jnp.max(past_scores, axis=-1), jnp.max(fresh_scores, axis=-1))[..., None]
    past_exp = jnp.exp(past_scores - highest)
    fresh_exp = jnp.exp(fresh_scores - highest)
    totals = jnp.sum(past_exp, axis=-1, keepdims=True) + jnp.sum(fresh_exp, axis=-1, keepdims=True)
    past_weights = (past_exp / totals).astype(jnp.bfloat16)
    fresh_weights = (fresh_exp / totals).astype(jnp.bfloat16)
    context = jnp.einsum(
        "ckgtp,cpkd->ctkgd", past_weights, stored_values, preferred_element_type=jnp.float32
    )
    context = context + jnp.einsum(
        "ckgts,cskd->ctkgd", fresh_weights, fresh_values, preferred_element_type=jnp.float32
    )
    return context.astype(jnp.bfloat16).reshape(span_count * window, kv_local * group * HD)


def a2a_sum(x, axis, dim, count):
    shape = x.shape
    split = shape[:dim] + (count, shape[dim] // count) + shape[dim + 1:]
    received = lax.all_to_all(x.reshape(split), axis, split_axis=dim, concat_axis=dim, tiled=True)
    return jnp.sum(received, axis=dim)


def a2a_gather(x, axis, count):
    spread = jnp.broadcast_to(x[None], (count,) + x.shape)
    return lax.all_to_all(spread, axis, split_axis=0, concat_axis=0, tiled=True)


def dp_gather(x, axis):
    return lax.all_gather(lax.all_gather(x, "y", axis=axis, tiled=True), "z", axis=axis, tiled=True)


def doubling_sum(x, axis, count):
    step = 1
    while step < count:
        x = x + lax.ppermute(x, axis, [(a, a ^ step) for a in range(count)])
        step *= 2
    return x


def shards(
    residual,
    queries,
    new_keys,
    new_values,
    cache_keys,
    cache_values,
    out_weight,
    ffn_gain,
    router,
    routes,
    w_gate,
    w_up,
    w_down,
    summary_gain,
    reduce_scale,
    assign,
):
    expert_count = lax.axis_size("expert")
    dp_index = lax.axis_index(DP)
    column = lax.axis_index("expert")
    span_local = cache_keys.shape[0]
    tok_local = residual.shape[0]
    width = residual.shape[1]
    slice_width = width // expert_count
    f32_precision = lax.Precision.HIGH
    attended = attend(queries, new_keys, new_values, cache_keys, cache_values)
    y_count = lax.axis_size("y")
    z_count = lax.axis_size("z")
    attended_row = lax.all_gather(attended, "y", axis=0, tiled=True)
    weight_row = a2a_gather(out_weight, "z", z_count)
    col_block = out_weight.shape[1]
    head_terms = jnp.einsum(
        "th,zhc->tzc", attended_row, weight_row, preferred_element_type=jnp.float32
    )
    head_terms = head_terms.reshape(y_count * expert_count, tok_local, z_count * col_block)
    token_cols = lax.all_to_all(
        head_terms, ("y", "expert"), split_axis=0, concat_axis=0, tiled=True
    )
    token_cols = jnp.sum(
        token_cols.reshape(y_count, expert_count, tok_local, z_count * col_block), axis=1
    )
    token_cols = token_cols.reshape(y_count, tok_local, z_count, col_block).transpose(1, 2, 0, 3)
    mixed = residual.astype(jnp.float32) + token_cols.reshape(tok_local, width)
    normed = (
        mixed * lax.rsqrt(jnp.mean(mixed * mixed, axis=-1, keepdims=True) + EPSILON) * ffn_gain
    ).astype(jnp.bfloat16)
    expert_ids = jnp.arange(EXPERTS, dtype=jnp.int32)
    first = routes[:, 0:1] == expert_ids[None, :]
    second = routes[:, 1:2] == expert_ids[None, :]
    partner = jnp.where(first, routes[:, 1:2], jnp.where(second, routes[:, 0:1], -1))
    tag_width = 128
    tag = jnp.broadcast_to(((partner + 1).T)[:, :, None], partner.T.shape + (tag_width,))
    outgoing = jnp.concatenate(
        [jnp.where((partner >= 0).T[:, :, None], normed[None, :, :], 0), tag.astype(jnp.bfloat16)],
        axis=2,
    )
    arrived = lax.all_to_all(outgoing, "expert", split_axis=0, concat_axis=1, tiled=True)
    arrived_rows = arrived[:, :, :width]
    arrived_partner = arrived[:, :, width].astype(jnp.int32) - 1
    present = (arrived_partner >= 0).astype(jnp.int32)
    position = jnp.cumsum(present, axis=1) - 1
    picker = (present[:, None, :] > 0) & (
        position[:, None, :] == jnp.arange(GROUP_CAP)[None, :, None]
    )
    compact = jnp.einsum(
        "eks,esd->ked",
        picker.astype(jnp.bfloat16),
        arrived_rows,
        preferred_element_type=jnp.float32,
    ).astype(jnp.bfloat16)
    arrived_count = arrived_partner.shape[1]
    pick = picker[0]
    slot_present = jnp.any(pick, axis=1)
    slot_partner = jnp.sum(jnp.where(pick, arrived_partner[0][None, :], 0), axis=1)
    local_span = jnp.arange(arrived_count) // WIN
    slot_span = jnp.sum(jnp.where(pick, local_span[None, :], 0), axis=1)
    slot_logits = jnp.dot(compact[:, 0, :], router, preferred_element_type=jnp.float32)
    own_logit = jnp.sum(jnp.where(expert_ids[None, :] == column, slot_logits, 0.0), axis=-1)
    partner_logit = jnp.sum(
        jnp.where(expert_ids[None, :] == slot_partner[:, None], slot_logits, 0.0), axis=-1
    )
    slot_gate = jnp.where(slot_present, jax.nn.sigmoid(own_logit - partner_logit), 0.0)
    pool_weight = jnp.where(
        slot_span[:, None] == jnp.arange(span_local)[None, :], slot_gate[:, None], 0.0
    )
    gathered = dp_gather(compact, 0)
    gathered_weight = lax.all_gather(pool_weight, DP, axis=0, tiled=True)
    n_dp = gathered.shape[0] // GROUP_CAP
    gate_proj = jnp.einsum("ned,edf->nf", gathered, w_gate, preferred_element_type=jnp.float32)
    up_proj = jnp.einsum("ned,edf->nf", gathered, w_up, preferred_element_type=jnp.float32)
    hidden = (jax.nn.silu(gate_proj) * up_proj).astype(jnp.bfloat16)
    span_hidden = jnp.einsum(
        "iks,ikf->isf",
        gathered_weight.reshape(n_dp, GROUP_CAP, span_local),
        hidden.reshape(n_dp, GROUP_CAP, -1).astype(jnp.float32),
        precision=f32_precision,
    ).reshape(n_dp * span_local, -1)
    pooled_part = jnp.dot(
        span_hidden, w_down[0].astype(jnp.float32), precision=f32_precision
    )
    own_span = dp_index * span_local + (column * tok_local) // WIN
    span_count = n_dp * span_local
    mixed_sum = jnp.sum(mixed, axis=0)
    pooled_part = pooled_part + jnp.where(
        (jnp.arange(span_count) == own_span)[:, None], mixed_sum[None, :], 0.0
    )
    pooled_cols = a2a_sum(pooled_part, "expert", 1, expert_count)
    own_cols = a2a_sum(pooled_cols, DP, 0, n_dp)
    squares = jnp.sum(
        a2a_gather(jnp.sum(own_cols * own_cols, axis=-1), "expert", expert_count), axis=0
    )
    summary = (
        own_cols * lax.rsqrt(squares / width + EPSILON)[:, None] * summary_gain
    ).astype(jnp.bfloat16)
    everyone = a2a_gather(summary, DP, n_dp).reshape(n_dp * span_local, slice_width)
    heads_local = slice_width // HD
    mine = summary.reshape(span_local, heads_local, HD)
    others = everyone.reshape(everyone.shape[0], heads_local, HD)
    factor = reduce_scale / math.sqrt(HD)
    scores = (
        jnp.einsum("chd,khd->hck", mine, others, preferred_element_type=jnp.float32)
        * factor[:, None, None]
    )
    own_assign = lax.dynamic_slice_in_dim(assign, dp_index * span_local, span_local)
    same = own_assign[:, None] == assign[None, :]
    scores = jnp.where(same[None], scores, -jnp.inf)
    highest = jnp.max(scores, axis=-1, keepdims=True)
    expo = jnp.exp(scores - highest)
    weights = (expo / jnp.sum(expo, axis=-1, keepdims=True)).astype(jnp.bfloat16)
    reduced = jnp.einsum("hck,khd->chd", weights, others, preferred_element_type=jnp.float32)
    reduced = reduced.reshape(span_local, slice_width).astype(jnp.bfloat16)
    return (summary, reduced)


def solution(mesh):
    dp_size, expert_size = mesh.devices.shape
    y_size = 4
    split_mesh = jax.sharding.Mesh(
        mesh.devices.reshape(dp_size // y_size, y_size, expert_size), ("z", "y", "expert")
    )
    return jax.shard_map(
        shards,
        mesh=split_mesh,
        in_specs=(
            P((*DP, "expert"), None),
            P(DP, "expert"),
            P(DP, "expert"),
            P(DP, "expert"),
            P(DP, None, "expert"),
            P(DP, None, "expert"),
            P("expert", DP),
            P(),
            P(),
            P((*DP, "expert"), None),
            P("expert", None, DP),
            P("expert", None, DP),
            P("expert", DP, None),
            P("expert"),
            P("expert"),
            P(),
        ),
        out_specs=(P(DP, "expert"), P(DP, "expert")),
        check_vma=False,
    )
```
